128 devices in a mesh: seq: 16 (over x, y), chan: 8 (over z, core).
Axes of the slice: x: 4, y: 4, z: 4, core: 2. Of those that a mesh axis runs over, the one named last changes fastest.
Arguments:
- hyena_query: bfloat16 [4096, 8192], P('seq', 'chan'), may hold values from -6 to 6
- hyena_key: bfloat16 [4096, 8192], P('seq', 'chan'), may hold values from -6 to 6
- hyena_value: bfloat16 [4096, 8192], P('seq', 'chan'), may hold values from -6 to 6
- bias: float32 [8192], P('chan'), may hold values from 0.5 to 1.5
- groups: int32 [8192], P('chan'), may hold values from 0 to 511
- filters: float32 [512, 4096], P('chan', 'seq'), may hold values from -1.5 to 1.5
- att_queries: bfloat16 [4096, 8192], P('seq', 'chan'), may hold values from -45 to 45
- att_keys: bfloat16 [4096, 8192], P('seq', 'chan'), may hold values from -5 to 5
- block_mask: int32 [32, 32], P('seq'), may hold values from 0 to 1, as said below
Outputs:
- hyena_out: bfloat16 [4096, 8192], P('seq', 'chan')
- attn_out: bfloat16 [4096, 8192], P('seq', 'chan')
The draws below stay inside these ranges and needn't reach their ends.
Inputs may be any that keep to these rules, and one draw needn't show every extreme that they name: block_mask[i, i] = 1 and block_mask[i, j] = 0 for j > i.
All inputs are finite; a program needn't handle non-finite values.
Results may differ from the reference program's by a relative error of at most 0.014.
Values may be sent and summed in bfloat16 or wider, within the bound.
No kernel may reach another device: no remote copies, remote signals or barrier semaphores. Data moves between devices by JAX's collectives and lax.ppermute only.
A program may use at most 128 MiB of HBM per device.

```python
import math
import jax
import jax.numpy as jnp
from jax import lax

D = 8192
HD = 128
HEADS = 64
FGROUPS = 512
ABLK = 128
TOKENS = 4096
NBLK = 32
N_CHAN = 8


def draw_filters(key, part):
    base = jax.random.fold_in(key, 3)
    key_noise, key_rate = jax.random.split(base)
    lengths = jnp.exp(jax.random.uniform(key_rate, (FGROUPS, 1), jnp.float32, math.log(40.0), math.log(4.0 * TOKENS)))
    noise = jnp.clip(jax.random.normal(key_noise, (FGROUPS, TOKENS), jnp.float32), -5.0, 5.0)
    effective = jnp.minimum(lengths, 1.0 * TOKENS)
    amplitude = jnp.sqrt(2.0 / effective)
    lags = jnp.arange(TOKENS, dtype=jnp.float32)[None, :]
    return noise * amplitude * jnp.exp(-lags / lengths)


def shared_keys(key):
    base = jax.random.fold_in(key, 7)
    key_main = jax.random.fold_in(base, 0)
    keys = jnp.clip(jax.random.normal(key_main, (TOKENS, D), jnp.float32), -4.0, 4.0)
    return keys


def draw_att_keys(key, part):
    return shared_keys(key).astype(jnp.bfloat16)


def draw_att_queries(key, part):
    key_query = jax.random.fold_in(key, 11)
    key_main = jax.random.fold_in(key_query, 0)
    queries = jnp.clip(jax.random.normal(key_main, (TOKENS, D), jnp.float32), -4.0, 4.0)
    return queries.astype(jnp.bfloat16)


def draw_block_mask(key, part):
    base = jax.random.fold_in(key, 5)
    coins = jax.random.randint(base, (NBLK, NBLK), 0, 2)
    row_index = jnp.arange(NBLK, dtype=jnp.int32)[:, None]
    col_index = jnp.arange(NBLK, dtype=jnp.int32)[None, :]
    return jnp.where(col_index < row_index, coins, jnp.where(col_index == row_index, 1, 0)).astype(jnp.int32)


def plant(entries, key, least, top_value):
    dims = entries.shape
    index_at = [jax.random.randint(jax.random.fold_in(key, axis), (), 0, dims[axis]) for axis in range(len(dims))]
    entries = entries.at[tuple(index_at)].set(least)
    longest = dims.index(max(dims))
    index_at[longest] = (index_at[longest] + 1) % dims[longest]
    return entries.at[tuple(index_at)].set(top_value)


def block_levels(stream_key, extent, cuts, low, top_value):
    loudness = 1.0
    for position, parts in cuts:
        draws = jax.random.uniform(jax.random.fold_in(jax.random.fold_in(stream_key, 6), position), (parts,), jnp.float32, low / len(cuts), top_value / len(cuts))
        loudness = loudness * jnp.repeat(jnp.exp(draws), extent[position] // parts).reshape((-1,) + (1,) * (len(extent) - 1 - position))
    return loudness


def scatter_about(key, dims, spread, limit, cuts=(), held_as=jnp.bfloat16):
    gain = block_levels(key, dims, cuts, -0.22, 0.18) if cuts else 1.0
    result = jax.random.normal(key, dims, jnp.float32) * spread * gain
    return jnp.minimum(jnp.maximum(result, -limit), limit).astype(held_as)


def setup_inputs(seed: int = 0) -> dict:
    arg_keys = jax.random.split(jax.random.key(seed), 10)
    hyena_query = scatter_about(arg_keys[0], (TOKENS, D), 1.0, 6.0, ((0, 16), (1, 8)))
    hyena_key = scatter_about(arg_keys[1], (TOKENS, D), 1.0, 6.0, ((0, 16), (1, 8)))
    hyena_value = scatter_about(arg_keys[2], (TOKENS, D), 1.0, 6.0, ((0, 16), (1, 8)))
    bias = jnp.clip(0.5 + 1.0 * jax.random.uniform(arg_keys[3], (D,), jnp.float32) ** block_levels(arg_keys[3], (D,), ((0, 8),), -0.2, 0.2), 0.5, 1.5)
    groups = plant(jax.random.randint(arg_keys[4], (D,), 0, FGROUPS), jax.random.fold_in(arg_keys[4], 1), 0, FGROUPS - 1).astype(jnp.int32)
    filters = draw_filters(jax.random.fold_in(arg_keys[9], 71), 0)
    att_queries = draw_att_queries(jax.random.fold_in(arg_keys[9], 71), 0)
    att_keys = draw_att_keys(jax.random.fold_in(arg_keys[9], 71), 0)
    block_mask = draw_block_mask(jax.random.fold_in(arg_keys[9], 71), 0)
    return dict(hyena_query=hyena_query, hyena_key=hyena_key, hyena_value=hyena_value, bias=bias, groups=groups, filters=filters, att_queries=att_queries, att_keys=att_keys, block_mask=block_mask)


def reference(hyena_query, hyena_key, hyena_value, bias, groups, filters, att_queries, att_keys, block_mask):
    mixed = (hyena_key.astype(jnp.float32) * hyena_value.astype(jnp.float32)).astype(jnp.bfloat16)
    values = mixed.astype(jnp.float32)
    width = D // N_CHAN
    blocks = values.reshape(TOKENS, N_CHAN, width).transpose(1, 0, 2)
    group_blocks = groups.reshape(N_CHAN, width)

    def convolve(pair):
        signal, chosen = pair
        kernel = filters[chosen].T
        spectrum = jnp.fft.rfft(signal, n=2 * TOKENS, axis=0) * jnp.fft.rfft(kernel, n=2 * TOKENS, axis=0)
        return jnp.fft.irfft(spectrum, n=2 * TOKENS, axis=0)[:TOKENS]

    conv = lax.map(convolve, (blocks, group_blocks)).transpose(1, 0, 2).reshape(TOKENS, D)
    hyena_out = (hyena_query.astype(jnp.float32) * (conv + bias[None, :] * values)).astype(jnp.bfloat16)

    positions = jnp.arange(TOKENS, dtype=jnp.int32)
    block_ids = positions // ABLK
    allowed = (block_mask[block_ids[:, None], block_ids[None, :]] == 1) & (positions[None, :] <= positions[:, None])
    queries = att_queries.reshape(TOKENS, HEADS, HD).transpose(1, 0, 2)
    keys = att_keys.reshape(TOKENS, HEADS, HD).transpose(1, 0, 2)
    heads_values = hyena_out.reshape(TOKENS, HEADS, HD).transpose(1, 0, 2)

    def one_head(triple):
        query_head, key_head, value_head = triple
        scores = jnp.dot(query_head, key_head.T, preferred_element_type=jnp.float32) * (HD ** -0.5)
        masked = jnp.where(allowed, scores, -jnp.inf)
        largest = jnp.max(masked, axis=-1, keepdims=True)
        weights = jnp.where(allowed, jnp.exp(masked - largest), 0.0)
        totals = jnp.sum(weights, axis=-1, keepdims=True)
        return jnp.dot(weights.astype(jnp.bfloat16), value_head, preferred_element_type=jnp.float32) / totals

    attended = lax.map(one_head, (queries, keys, heads_values))
    attn_out = attended.transpose(1, 0, 2).reshape(TOKENS, D).astype(jnp.bfloat16)
    return hyena_out, attn_out
```

```python
import math

import numpy as np

import jax
import jax.numpy as jnp
from jax import lax
from jax.sharding import PartitionSpec as P

HD = 128
ABLK = 128

dft_precision = lax.Precision.HIGH


def dft_tables(length):
    total = 2 * length
    outer = 64
    inner = total // outer
    used = length // outer
    k_in = np.arange(inner)[:, None]
    n_out = np.arange(used)[None, :]
    angle_b = 2.0 * np.pi * k_in * n_out / inner
    k_a = np.arange(outer)[:, None]
    n_a = np.arange(outer)[None, :]
    angle_a = 2.0 * np.pi * k_a * n_a / outer
    angle_t = 2.0 * np.pi * np.arange(inner)[:, None] * np.arange(outer)[None, :] / total
    f32 = lambda a: jnp.asarray(a.astype(np.float32))
    return dict(
        cos_b=f32(np.cos(angle_b)),
        sin_b=f32(np.sin(angle_b)),
        cos_a=f32(np.cos(angle_a)),
        sin_a=f32(np.sin(angle_a)),
        cos_t=f32(np.cos(angle_t)),
        sin_t=f32(np.sin(angle_t)),
        inv_cos_b=f32(np.cos(angle_b).T / total),
        inv_sin_b=f32(np.sin(angle_b).T / total),
        outer=outer,
        used=used,
    )


def mm(spec, a, b):
    return jnp.einsum(spec, a, b, precision=dft_precision, preferred_element_type=jnp.float32)


def forward_dft(signal, tab):
    length, channels = signal.shape
    outer, used = tab["outer"], tab["used"]
    data = signal.reshape(used, outer, channels)
    y_re = mm("kn,nmc->kmc", tab["cos_b"], data)
    y_im = -mm("kn,nmc->kmc", tab["sin_b"], data)
    tc = tab["cos_t"][:, :, None]
    ts = tab["sin_t"][:, :, None]
    t_re = y_re * tc + y_im * ts
    t_im = y_im * tc - y_re * ts
    x_re = mm("an,knc->akc", tab["cos_a"], t_re) + mm("an,knc->akc", tab["sin_a"], t_im)
    x_im = mm("an,knc->akc", tab["cos_a"], t_im) - mm("an,knc->akc", tab["sin_a"], t_re)
    return x_re, x_im


def inverse_dft(p_re, p_im, tab):
    outer, inner, channels = p_re.shape
    z_re = mm("tk,kqc->tqc", tab["cos_a"], p_re) - mm("tk,kqc->tqc", tab["sin_a"], p_im)
    z_im = mm("tk,kqc->tqc", tab["cos_a"], p_im) + mm("tk,kqc->tqc", tab["sin_a"], p_re)
    tc = tab["cos_t"].T[:, :, None]
    ts = tab["sin_t"].T[:, :, None]
    w_re = z_re * tc - z_im * ts
    w_im = z_re * ts + z_im * tc
    out = mm("sq,tqc->stc", tab["inv_cos_b"], w_re) - mm("sq,tqc->stc", tab["inv_sin_b"], w_im)
    return out.reshape(tab["used"] * outer, channels)


def to_columns(block, pieces):
    rows, width = block.shape
    send = block.reshape(rows, pieces, width // pieces).transpose(1, 0, 2)
    got = lax.all_to_all(send, "seq", 0, 0, tiled=True)
    return got.reshape(pieces * rows, width // pieces)


def to_rows(block, pieces):
    total, width = block.shape
    rows = total // pieces
    send = block.reshape(pieces, rows, width)
    got = lax.all_to_all(send, "seq", 0, 0, tiled=True)
    return got.reshape(pieces, rows, width).transpose(1, 0, 2).reshape(rows, pieces * width)


def on_device(
    hyena_query, hyena_key, hyena_value, bias, groups, filters, att_queries, att_keys, block_mask
):
    rows_dev, channels = hyena_query.shape
    pieces = lax.axis_size("seq")
    device = lax.axis_index("seq")
    length = rows_dev * pieces
    width = channels // pieces
    tab = dft_tables(length)

    mixed = (hyena_key.astype(jnp.float32) * hyena_value.astype(jnp.float32)).astype(jnp.bfloat16)
    mixed_cols = to_columns(mixed, pieces)
    query_cols = to_columns(hyena_query, pieces)

    bank = lax.all_gather(filters.astype(jnp.bfloat16), "chan", axis=0, tiled=True)
    picked = jnp.take(bank, groups.reshape(pieces, width), axis=0)
    lag_parts = lax.all_to_all(picked, "seq", 0, 0, tiled=True)
    lag_parts = lag_parts.reshape(pieces, width, rows_dev)
    kernel = lag_parts.transpose(0, 2, 1).reshape(length, width).astype(jnp.float32)

    values = mixed_cols.astype(jnp.float32)
    s_re, s_im = forward_dft(values, tab)
    f_re, f_im = forward_dft(kernel, tab)
    conv = inverse_dft(s_re * f_re - s_im * f_im, s_re * f_im + s_im * f_re, tab)
    bias_here = lax.dynamic_slice_in_dim(bias, device * width, width)
    out_cols = (
        query_cols.astype(jnp.float32) * (conv + bias_here[None, :] * values)
    ).astype(jnp.bfloat16)
    hyena_out = to_rows(out_cols, pieces)

    attn_out = attention(att_queries, att_keys, out_cols, block_mask, pieces, device)
    return (hyena_out, attn_out)


def attention(att_queries, att_keys, value_half, block_mask, pieces, device):
    rows_dev, channels = att_queries.shape
    heads = channels // HD
    length = rows_dev * pieces
    sub = rows_dev // ABLK
    parity = device % sub
    head = device // sub

    queries = att_queries.reshape(sub, ABLK, heads, HD).transpose(2, 0, 1, 3)
    queries = queries.reshape(heads * sub, ABLK, HD)
    q_here = lax.all_to_all(queries, "seq", 0, 0, tiled=True).reshape(pieces * ABLK, HD)

    keys = att_keys.reshape(rows_dev, heads, 1, HD).transpose(1, 2, 0, 3)
    keys = jnp.broadcast_to(keys, (heads, sub, rows_dev, HD)).reshape(heads * sub, rows_dev, HD)
    k_here = lax.all_to_all(keys, "seq", 0, 0, tiled=True).reshape(length, HD)

    pairs = [(source, source ^ 1) for source in range(pieces)]
    other_half = lax.ppermute(value_half, "seq", pairs)
    first = jnp.where(parity == 0, value_half, other_half)
    second = jnp.where(parity == 0, other_half, value_half)
    v_here = jnp.concatenate([first, second], axis=1)

    full_mask = lax.all_gather(block_mask, "seq", axis=0, tiled=True)
    block_count = full_mask.shape[0]
    q_blocks = sub * jnp.arange(pieces, dtype=jnp.int32) + parity
    mask_rows = jnp.take(full_mask, q_blocks, axis=0)
    query_pos = (q_blocks[:, None] * ABLK + jnp.arange(ABLK, dtype=jnp.int32)[None, :]).reshape(-1)
    key_pos = jnp.arange(length, dtype=jnp.int32)
    block_ok = jnp.repeat(jnp.repeat(mask_rows, ABLK, axis=0), ABLK, axis=1) == 1
    allowed = block_ok & (key_pos[None, :] <= query_pos[:, None])

    scale = HD ** (-0.5)
    scores = jnp.dot(q_here, k_here.T, preferred_element_type=jnp.float32) * scale
    scores = jnp.where(allowed, scores, -1e30)
    largest = jnp.max(scores, axis=-1, keepdims=True)
    weights = jnp.where(allowed, jnp.exp(scores - largest), 0.0)
    totals = jnp.sum(weights, axis=-1, keepdims=True)
    acc = jnp.dot(weights.astype(jnp.bfloat16), v_here, preferred_element_type=jnp.float32)
    result = (acc / totals).astype(jnp.bfloat16)

    back = lax.all_to_all(result.reshape(pieces, ABLK, HD), "seq", 0, 0, tiled=True)
    back = back.reshape(heads, sub, ABLK, HD).transpose(1, 2, 0, 3)
    return back.reshape(rows_dev, channels)


def solution(mesh):
    return jax.shard_map(
        on_device,
        mesh=mesh,
        in_specs=(
            P("seq", "chan"),
            P("seq", "chan"),
            P("seq", "chan"),
            P("chan"),
            P("chan"),
            P("chan", "seq"),
            P("seq", "chan"),
            P("seq", "chan"),
            P("seq", None),
        ),
        out_specs=(P("seq", "chan"), P("seq", "chan")),
        check_vma=False,
    )
```

```python
import math

import numpy as np

import jax
import jax.numpy as jnp
from jax import lax
from jax.sharding import PartitionSpec as P

HD = 128
ABLK = 128

dft_precision = lax.Precision.HIGH


def dft_tables(length):
    total = 2 * length
    outer = 64
    inner = total // outer
    used = length // outer
    k_in = np.arange(inner)[:, None]
    n_out = np.arange(used)[None, :]
    angle_b = 2.0 * np.pi * k_in * n_out / inner
    k_a = np.arange(outer)[:, None]
    n_a = np.arange(outer)[None, :]
    angle_a = 2.0 * np.pi * k_a * n_a / outer
    angle_t = 2.0 * np.pi * np.arange(inner)[:, None] * np.arange(outer)[None, :] / total
    f32 = lambda a: jnp.asarray(a.astype(np.float32))
    return dict(
        cos_b=f32(np.cos(angle_b)),
        sin_b=f32(np.sin(angle_b)),
        cos_a=f32(np.cos(angle_a)),
        sin_a=f32(np.sin(angle_a)),
        cos_t=f32(np.cos(angle_t)),
        sin_t=f32(np.sin(angle_t)),
        inv_cos_b=f32(np.cos(angle_b).T / total),
        inv_sin_b=f32(np.sin(angle_b).T / total),
        outer=outer,
        used=used,
    )


def mm(spec, a, b):
    return jnp.einsum(spec, a, b, precision=dft_precision, preferred_element_type=jnp.float32)


def forward_dft(signal, tab):
    length, channels = signal.shape
    outer, used = tab["outer"], tab["used"]
    data = signal.reshape(used, outer, channels)
    y_re = mm("kn,nmc->kmc", tab["cos_b"], data)
    y_im = -mm("kn,nmc->kmc", tab["sin_b"], data)
    tc = tab["cos_t"][:, :, None]
    ts = tab["sin_t"][:, :, None]
    t_re = y_re * tc + y_im * ts
    t_im = y_im * tc - y_re * ts
    x_re = mm("an,knc->akc", tab["cos_a"], t_re) + mm("an,knc->akc", tab["sin_a"], t_im)
    x_im = mm("an,knc->akc", tab["cos_a"], t_im) - mm("an,knc->akc", tab["sin_a"], t_re)
    return x_re, x_im


def inverse_dft(p_re, p_im, tab):
    outer, inner, channels = p_re.shape
    z_re = mm("tk,kqc->tqc", tab["cos_a"], p_re) - mm("tk,kqc->tqc", tab["sin_a"], p_im)
    z_im = mm("tk,kqc->tqc", tab["cos_a"], p_im) + mm("tk,kqc->tqc", tab["sin_a"], p_re)
    tc = tab["cos_t"].T[:, :, None]
    ts = tab["sin_t"].T[:, :, None]
    w_re = z_re * tc - z_im * ts
    w_im = z_re * ts + z_im * tc
    out = mm("sq,tqc->stc", tab["inv_cos_b"], w_re) - mm("sq,tqc->stc", tab["inv_sin_b"], w_im)
    return out.reshape(tab["used"] * outer, channels)


def to_columns(block, pieces):
    rows, width = block.shape
    send = block.reshape(rows, pieces, width // pieces).transpose(1, 0, 2)
    got = lax.all_to_all(send, "seq", 0, 0, tiled=True)
    return got.reshape(pieces * rows, width // pieces)


def to_rows(block, pieces):
    total, width = block.shape
    rows = total // pieces
    send = block.reshape(pieces, rows, width)
    got = lax.all_to_all(send, "seq", 0, 0, tiled=True)
    return got.reshape(pieces, rows, width).transpose(1, 0, 2).reshape(rows, pieces * width)


def on_device(
    hyena_query, hyena_key, hyena_value, bias, groups, filters, att_queries, att_keys, block_mask
):
    rows_dev, channels = hyena_query.shape
    pieces = lax.axis_size("seq")
    device = lax.axis_index("seq")
    length = rows_dev * pieces
    width = channels // pieces
    tab = dft_tables(length)

    mixed = (hyena_key.astype(jnp.float32) * hyena_value.astype(jnp.float32)).astype(jnp.bfloat16)
    bank = lax.all_gather(filters.astype(jnp.bfloat16), "chan", axis=0, tiled=True)
    picked = jnp.take(bank, groups.reshape(pieces, width), axis=0).transpose(0, 2, 1)
    sends = [
        part.reshape(rows_dev, pieces, width).transpose(1, 0, 2) for part in (mixed, hyena_query)
    ]
    got = lax.all_to_all(jnp.concatenate(sends + [picked], axis=2), "seq", 0, 0, tiled=True)
    mixed_cols = got[:, :, :width].reshape(length, width)
    query_cols = got[:, :, width : 2 * width].reshape(length, width)
    kernel = got[:, :, 2 * width :].reshape(length, width).astype(jnp.float32)

    values = mixed_cols.astype(jnp.float32)
    s_re, s_im = forward_dft(values, tab)
    f_re, f_im = forward_dft(kernel, tab)
    conv = inverse_dft(s_re * f_re - s_im * f_im, s_re * f_im + s_im * f_re, tab)
    bias_here = lax.dynamic_slice_in_dim(bias, device * width, width)
    out_cols = (
        query_cols.astype(jnp.float32) * (conv + bias_here[None, :] * values)
    ).astype(jnp.bfloat16)
    hyena_out = to_rows(out_cols, pieces)

    attn_out = attention(att_queries, att_keys, out_cols, block_mask, pieces, device)
    return (hyena_out, attn_out)


def attention(att_queries, att_keys, value_half, block_mask, pieces, device):
    rows_dev, channels = att_queries.shape
    heads = channels // HD
    length = rows_dev * pieces
    sub = rows_dev // ABLK
    parity = device % sub
    head = device // sub

    block_count = block_mask.shape[1]
    queries = att_queries.reshape(sub, ABLK, heads, HD).transpose(2, 0, 1, 3)
    keys = att_keys.reshape(rows_dev, heads, 1, HD).transpose(1, 2, 0, 3)
    keys = jnp.broadcast_to(keys, (heads, sub, rows_dev, HD))
    mask_pad = jnp.zeros((sub, 8, HD), jnp.bfloat16).at[:, 0, :block_count].set(
        block_mask.astype(jnp.bfloat16)
    )
    mask_pad = jnp.broadcast_to(mask_pad[None], (heads, sub, 8, HD))
    payload = jnp.concatenate([keys, queries, mask_pad], axis=2)
    payload = payload.reshape(heads * sub, rows_dev + ABLK + 8, HD)
    got = lax.all_to_all(payload, "seq", 0, 0, tiled=True)
    k_here = got[:, :rows_dev].reshape(length, HD)
    q_here = got[:, rows_dev : rows_dev + ABLK].reshape(pieces * ABLK, HD)
    mask_rows = got[:, rows_dev + ABLK, :block_count] > 0.5

    pairs = [(source, source ^ 1) for source in range(pieces)]
    other_half = lax.ppermute(value_half, "seq", pairs)
    first = jnp.where(parity == 0, value_half, other_half)
    second = jnp.where(parity == 0, other_half, value_half)
    v_here = jnp.concatenate([first, second], axis=1)

    scale = HD ** (-0.5)
    q_blocks = sub * jnp.arange(pieces, dtype=jnp.int32) + parity
    query_pos = (q_blocks[:, None] * ABLK + jnp.arange(ABLK, dtype=jnp.int32)[None, :]).reshape(-1)
    group_count = 4
    per_group = pieces // group_count
    outs = []
    for g in range(group_count):
        rows = slice(g * per_group * ABLK, (g + 1) * per_group * ABLK)
        key_len = length * (g + 1) // group_count
        key_pos = jnp.arange(key_len, dtype=jnp.int32)
        block_ok = mask_rows[g * per_group : (g + 1) * per_group, : key_len // ABLK]
        block_ok = jnp.repeat(jnp.repeat(block_ok, ABLK, axis=0), ABLK, axis=1)
        allowed = block_ok & (key_pos[None, :] <= query_pos[rows][:, None])
        scores = jnp.dot(q_here[rows], k_here[:key_len].T, preferred_element_type=jnp.float32) * scale
        scores = jnp.where(allowed, scores, -1e30)
        largest = jnp.max(scores, axis=-1, keepdims=True)
        weights = jnp.where(allowed, jnp.exp(scores - largest), 0.0)
        totals = jnp.sum(weights, axis=-1, keepdims=True)
        acc = jnp.dot(
            weights.astype(jnp.bfloat16), v_here[:key_len], preferred_element_type=jnp.float32
        )
        outs.append(acc / totals)
    result = jnp.concatenate(outs, axis=0).astype(jnp.bfloat16)

    back = lax.all_to_all(result.reshape(pieces, ABLK, HD), "seq", 0, 0, tiled=True)
    back = back.reshape(heads, sub, ABLK, HD).transpose(1, 2, 0, 3)
    return back.reshape(rows_dev, channels)


def solution(mesh):
    return jax.shard_map(
        on_device,
        mesh=mesh,
        in_specs=(
            P("seq", "chan"),
            P("seq", "chan"),
            P("seq", "chan"),
            P("chan"),
            P("chan"),
            P("chan", "seq"),
            P("seq", "chan"),
            P("seq", "chan"),
            P("seq", None),
        ),
        out_specs=(P("seq", "chan"), P("seq", "chan")),
        check_vma=False,
    )
```

```python
import math

import numpy as np

import jax
import jax.numpy as jnp
from jax import lax
from jax.sharding import PartitionSpec as P

HD = 128
ABLK = 128

dft_precision = lax.Precision.DEFAULT


def dft_tables(length):
    total = 2 * length
    outer = 64
    inner = total // outer
    used = length // outer
    k_in = np.arange(inner)[:, None]
    n_out = np.arange(used)[None, :]
    angle_b = 2.0 * np.pi * k_in * n_out / inner
    k_a = np.arange(outer)[:, None]
    n_a = np.arange(outer)[None, :]
    angle_a = 2.0 * np.pi * k_a * n_a / outer
    angle_t = 2.0 * np.pi * np.arange(inner)[:, None] * np.arange(outer)[None, :] / total
    f32 = lambda a: jnp.asarray(a.astype(np.float32))
    return dict(
        cos_b=f32(np.cos(angle_b)),
        sin_b=f32(np.sin(angle_b)),
        cos_a=f32(np.cos(angle_a)),
        sin_a=f32(np.sin(angle_a)),
        cos_t=f32(np.cos(angle_t)),
        sin_t=f32(np.sin(angle_t)),
        inv_cos_b=f32(np.cos(angle_b).T / total),
        inv_sin_b=f32(np.sin(angle_b).T / total),
        outer=outer,
        used=used,
    )


def mm(spec, a, b):
    return jnp.einsum(spec, a, b, precision=dft_precision, preferred_element_type=jnp.float32)


def forward_dft(signal, tab):
    length, channels = signal.shape
    outer, used = tab["outer"], tab["used"]
    data = signal.reshape(used, outer, channels)
    y_re = mm("kn,nmc->kmc", tab["cos_b"], data)
    y_im = -mm("kn,nmc->kmc", tab["sin_b"], data)
    tc = tab["cos_t"][:, :, None]
    ts = tab["sin_t"][:, :, None]
    t_re = y_re * tc + y_im * ts
    t_im = y_im * tc - y_re * ts
    x_re = mm("an,knc->akc", tab["cos_a"], t_re) + mm("an,knc->akc", tab["sin_a"], t_im)
    x_im = mm("an,knc->akc", tab["cos_a"], t_im) - mm("an,knc->akc", tab["sin_a"], t_re)
    return x_re, x_im


def inverse_dft(p_re, p_im, tab):
    outer, inner, channels = p_re.shape
    z_re = mm("tk,kqc->tqc", tab["cos_a"], p_re) - mm("tk,kqc->tqc", tab["sin_a"], p_im)
    z_im = mm("tk,kqc->tqc", tab["cos_a"], p_im) + mm("tk,kqc->tqc", tab["sin_a"], p_re)
    tc = tab["cos_t"].T[:, :, None]
    ts = tab["sin_t"].T[:, :, None]
    w_re = z_re * tc - z_im * ts
    w_im = z_re * ts + z_im * tc
    out = mm("sq,tqc->stc", tab["inv_cos_b"], w_re) - mm("sq,tqc->stc", tab["inv_sin_b"], w_im)
    return out.reshape(tab["used"] * outer, channels)


def to_columns(block, pieces):
    rows, width = block.shape
    send = block.reshape(rows, pieces, width // pieces).transpose(1, 0, 2)
    got = lax.all_to_all(send, "seq", 0, 0, tiled=True)
    return got.reshape(pieces * rows, width // pieces)


def to_rows(block, pieces):
    total, width = block.shape
    rows = total // pieces
    send = block.reshape(pieces, rows, width)
    got = lax.all_to_all(send, "seq", 0, 0, tiled=True)
    return got.reshape(pieces, rows, width).transpose(1, 0, 2).reshape(rows, pieces * width)


def on_device(
    hyena_query, hyena_key, hyena_value, bias, groups, filters, att_queries, att_keys, block_mask
):
    rows_dev, channels = hyena_query.shape
    pieces = lax.axis_size("seq")
    device = lax.axis_index("seq")
    length = rows_dev * pieces
    width = channels // pieces
    tab = dft_tables(length)

    mixed = (hyena_key.astype(jnp.float32) * hyena_value.astype(jnp.float32)).astype(jnp.bfloat16)
    bank = lax.all_gather(filters.astype(jnp.bfloat16), "chan", axis=0, tiled=True)
    picked = jnp.take(bank, groups.reshape(pieces, width), axis=0).transpose(0, 2, 1)
    sends = [
        part.reshape(rows_dev, pieces, width).transpose(1, 0, 2) for part in (mixed, hyena_query)
    ]
    got = lax.all_to_all(jnp.concatenate(sends + [picked], axis=2), "seq", 0, 0, tiled=True)
    mixed_cols = got[:, :, :width].reshape(length, width)
    query_cols = got[:, :, width : 2 * width].reshape(length, width)
    kernel = got[:, :, 2 * width :].reshape(length, width).astype(jnp.float32)

    values = mixed_cols.astype(jnp.float32)
    s_re, s_im = forward_dft(values, tab)
    f_re, f_im = forward_dft(kernel, tab)
    conv = inverse_dft(s_re * f_re - s_im * f_im, s_re * f_im + s_im * f_re, tab)
    bias_here = lax.dynamic_slice_in_dim(bias, device * width, width)
    out_cols = (
        query_cols.astype(jnp.float32) * (conv + bias_here[None, :] * values)
    ).astype(jnp.bfloat16)
    hyena_out = to_rows(out_cols, pieces)

    attn_out = attention(att_queries, att_keys, out_cols, block_mask, pieces, device)
    return (hyena_out, attn_out)


def attention(att_queries, att_keys, value_half, block_mask, pieces, device):
    rows_dev, channels = att_queries.shape
    heads = channels // HD
    length = rows_dev * pieces
    sub = rows_dev // ABLK
    parity = device % sub
    head = device // sub

    block_count = block_mask.shape[1]
    queries = att_queries.reshape(sub, ABLK, heads, HD).transpose(2, 0, 1, 3)
    keys = att_keys.reshape(rows_dev, heads, 1, HD).transpose(1, 2, 0, 3)
    keys = jnp.broadcast_to(keys, (heads, sub, rows_dev, HD))
    mask_pad = jnp.zeros((sub, 8, HD), jnp.bfloat16).at[:, 0, :block_count].set(
        block_mask.astype(jnp.bfloat16)
    )
    mask_pad = jnp.broadcast_to(mask_pad[None], (heads, sub, 8, HD))
    payload = jnp.concatenate([keys, queries, mask_pad], axis=2)
    payload = payload.reshape(heads * sub, rows_dev + ABLK + 8, HD)
    got = lax.all_to_all(payload, "seq", 0, 0, tiled=True)
    k_here = got[:, :rows_dev].reshape(length, HD)
    q_here = got[:, rows_dev : rows_dev + ABLK].reshape(pieces * ABLK, HD)
    mask_rows = got[:, rows_dev + ABLK, :block_count] > 0.5

    pairs = [(source, source ^ 1) for source in range(pieces)]
    other_half = lax.ppermute(value_half, "seq", pairs)
    first = jnp.where(parity == 0, value_half, other_half)
    second = jnp.where(parity == 0, other_half, value_half)
    v_here = jnp.concatenate([first, second], axis=1)

    scale = HD ** (-0.5)
    q_blocks = sub * jnp.arange(pieces, dtype=jnp.int32) + parity
    query_pos = (q_blocks[:, None] * ABLK + jnp.arange(ABLK, dtype=jnp.int32)[None, :]).reshape(-1)
    group_count = 8
    per_group = pieces // group_count
    outs = []
    for g in range(group_count):
        rows = slice(g * per_group * ABLK, (g + 1) * per_group * ABLK)
        key_len = length * (g + 1) // group_count
        kblocks = key_len // ABLK
        block_ok = mask_rows[g * per_group : (g + 1) * per_group, :kblocks]
        q_pos = query_pos[rows].reshape(per_group, ABLK)
        k_pos = jnp.arange(key_len, dtype=jnp.int32).reshape(kblocks, ABLK)
        allowed = block_ok[:, None, :, None] & (
            k_pos[None, None, :, :] <= q_pos[:, :, None, None]
        )
        scores = jnp.dot(q_here[rows], k_here[:key_len].T, preferred_element_type=jnp.float32) * scale
        scores = scores.reshape(per_group, ABLK, kblocks, ABLK)
        scores = jnp.where(allowed, scores, -1e30)
        largest = jnp.max(scores, axis=(2, 3), keepdims=True)
        weights = jnp.where(allowed, jnp.exp(scores - largest), 0.0)
        totals = jnp.sum(weights, axis=(2, 3)).reshape(per_group * ABLK, 1)
        weights = weights.reshape(per_group * ABLK, key_len).astype(jnp.bfloat16)
        acc = jnp.dot(weights, v_here[:key_len], preferred_element_type=jnp.float32)
        outs.append(acc / totals)
    result = jnp.concatenate(outs, axis=0).astype(jnp.bfloat16)

    back = lax.all_to_all(result.reshape(pieces, ABLK, HD), "seq", 0, 0, tiled=True)
    back = back.reshape(heads, sub, ABLK, HD).transpose(1, 2, 0, 3)
    return back.reshape(rows_dev, channels)


def solution(mesh):
    return jax.shard_map(
        on_device,
        mesh=mesh,
        in_specs=(
            P("seq", "chan"),
            P("seq", "chan"),
            P("seq", "chan"),
            P("chan"),
            P("chan"),
            P("chan", "seq"),
            P("seq", "chan"),
            P("seq", "chan"),
            P("seq", None),
        ),
        out_specs=(P("seq", "chan"), P("seq", "chan")),
        check_vma=False,
    )
```

```python
import math

import numpy as np

import jax
import jax.numpy as jnp
from jax import lax
from jax.sharding import PartitionSpec as P

HD = 128
ABLK = 128

dft_precision = lax.Precision.DEFAULT


def dft_tables(length):
    total = 2 * length
    lanes = 128
    outer = total // lanes
    used = length // lanes
    f32 = lambda a: jnp.asarray(a.astype(np.float32))
    angle_b = 2.0 * np.pi * np.arange(outer)[:, None] * np.arange(used)[None, :] / outer
    angle_a = 2.0 * np.pi * np.arange(lanes)[:, None] * np.arange(lanes)[None, :] / lanes
    angle_t = 2.0 * np.pi * np.arange(outer)[:, None] * np.arange(lanes)[None, :] / total
    return dict(
        cos_b=f32(np.cos(angle_b)),
        sin_b=f32(np.sin(angle_b)),
        cos_a=f32(np.cos(angle_a)),
        sin_a=f32(np.sin(angle_a)),
        cos_t=f32(np.cos(angle_t))[:, None, :],
        sin_t=f32(np.sin(angle_t))[:, None, :],
        inv_cos_b=f32(np.cos(angle_b).T / total),
        inv_sin_b=f32(np.sin(angle_b).T / total),
    )


def mm(spec, a, b):
    return jnp.einsum(spec, a, b, precision=dft_precision, preferred_element_type=jnp.float32)


def forward_dft(data, tab):
    y_re = mm("kn,ncm->kcm", tab["cos_b"], data)
    y_im = -mm("kn,ncm->kcm", tab["sin_b"], data)
    tc, ts = tab["cos_t"], tab["sin_t"]
    t_re = y_re * tc + y_im * ts
    t_im = y_im * tc - y_re * ts
    x_re = mm("kcm,am->kca", t_re, tab["cos_a"]) + mm("kcm,am->kca", t_im, tab["sin_a"])
    x_im = mm("kcm,am->kca", t_im, tab["cos_a"]) - mm("kcm,am->kca", t_re, tab["sin_a"])
    return x_re, x_im


def inverse_dft(p_re, p_im, tab):
    z_re = mm("kca,ta->kct", p_re, tab["cos_a"]) - mm("kca,ta->kct", p_im, tab["sin_a"])
    z_im = mm("kca,ta->kct", p_im, tab["cos_a"]) + mm("kca,ta->kct", p_re, tab["sin_a"])
    tc, ts = tab["cos_t"], tab["sin_t"]
    w_re = z_re * tc - z_im * ts
    w_im = z_re * ts + z_im * tc
    return mm("sk,kct->sct", tab["inv_cos_b"], w_re) - mm("sk,kct->sct", tab["inv_sin_b"], w_im)


def on_device(
    hyena_query, hyena_key, hyena_value, bias, groups, filters, att_queries, att_keys, block_mask
):
    rows_dev, channels = hyena_query.shape
    pieces = lax.axis_size("seq")
    device = lax.axis_index("seq")
    length = rows_dev * pieces
    width = channels // pieces
    tab = dft_tables(length)

    mixed = (hyena_key.astype(jnp.float32) * hyena_value.astype(jnp.float32)).astype(jnp.bfloat16)
    bank = lax.all_gather(filters.astype(jnp.bfloat16), "chan", axis=0, tiled=True)
    picked = jnp.take(bank, groups.reshape(pieces, width), axis=0)
    halves = rows_dev // 128
    picked = picked.reshape(pieces, width, halves, 128).transpose(0, 2, 1, 3)
    sends = [
        part.reshape(halves, 128, pieces, width).transpose(2, 0, 3, 1)
        for part in (mixed, hyena_query)
    ]
    got = lax.all_to_all(jnp.concatenate(sends + [picked], axis=2), "seq", 0, 0, tiled=True)
    got = got.reshape(pieces * halves, 3 * width, 128)
    mixed_cols = got[:, :width]
    query_cols = got[:, width : 2 * width]
    kernel = got[:, 2 * width :]

    s_re, s_im = forward_dft(mixed_cols, tab)
    f_re, f_im = forward_dft(kernel, tab)
    conv = inverse_dft(s_re * f_re - s_im * f_im, s_re * f_im + s_im * f_re, tab)
    bias_here = lax.dynamic_slice_in_dim(bias, device * width, width)
    out_cols = (
        query_cols.astype(jnp.float32)
        * (conv + bias_here[None, :, None] * mixed_cols.astype(jnp.float32))
    ).astype(jnp.bfloat16)
    back = lax.all_to_all(out_cols.reshape(pieces, halves, width, 128), "seq", 0, 0, tiled=True)
    hyena_out = back.transpose(1, 3, 0, 2).reshape(rows_dev, channels)
    value_t = out_cols.transpose(1, 0, 2).reshape(width, length)

    attn_out = attention(att_queries, att_keys, value_t, block_mask, pieces, device)
    return (hyena_out, attn_out)


def attention(att_queries, att_keys, value_half, block_mask, pieces, device):
    rows_dev, channels = att_queries.shape
    heads = channels // HD
    length = rows_dev * pieces
    sub = rows_dev // ABLK
    parity = device % sub
    head = device // sub

    block_count = block_mask.shape[1]
    queries = att_queries.reshape(sub, ABLK, heads, HD).transpose(2, 0, 1, 3)
    keys = att_keys.reshape(rows_dev, heads, 1, HD).transpose(1, 2, 0, 3)
    keys = jnp.broadcast_to(keys, (heads, sub, rows_dev, HD))
    mask_pad = jnp.zeros((sub, 8, HD), jnp.bfloat16).at[:, 0, :block_count].set(
        block_mask.astype(jnp.bfloat16)
    )
    mask_pad = jnp.broadcast_to(mask_pad[None], (heads, sub, 8, HD))
    payload = jnp.concatenate([keys, queries, mask_pad], axis=2)
    payload = payload.reshape(heads * sub, rows_dev + ABLK + 8, HD)
    got = lax.all_to_all(payload, "seq", 0, 0, tiled=True)
    k_here = got[:, :rows_dev].reshape(length, HD)
    q_here = got[:, rows_dev : rows_dev + ABLK].reshape(pieces * ABLK, HD)
    mask_rows = got[:, rows_dev + ABLK, :block_count] > 0.5

    pairs = [(source, source ^ 1) for source in range(pieces)]
    other_half = lax.ppermute(value_half, "seq", pairs)
    first = jnp.where(parity == 0, value_half, other_half)
    second = jnp.where(parity == 0, other_half, value_half)
    v_here = jnp.concatenate([first, second], axis=0)

    scale = HD ** (-0.5)
    q_blocks = sub * jnp.arange(pieces, dtype=jnp.int32) + parity
    query_pos = (q_blocks[:, None] * ABLK + jnp.arange(ABLK, dtype=jnp.int32)[None, :]).reshape(-1)
    group_count = 8
    per_group = pieces // group_count
    outs = []
    for g in range(group_count):
        rows = slice(g * per_group * ABLK, (g + 1) * per_group * ABLK)
        key_len = length * (g + 1) // group_count
        kblocks = key_len // ABLK
        block_ok = mask_rows[g * per_group : (g + 1) * per_group, :kblocks]
        q_pos = query_pos[rows].reshape(per_group, ABLK)
        k_pos = jnp.arange(key_len, dtype=jnp.int32).reshape(kblocks, ABLK)
        allowed = block_ok[:, None, :, None] & (
            k_pos[None, None, :, :] <= q_pos[:, :, None, None]
        )
        scores = jnp.dot(q_here[rows], k_here[:key_len].T, preferred_element_type=jnp.float32) * scale
        scores = scores.reshape(per_group, ABLK, kblocks, ABLK)
        scores = jnp.where(allowed, scores, -1e30)
        largest = jnp.max(scores, axis=(2, 3), keepdims=True)
        weights = jnp.where(allowed, jnp.exp(scores - largest), 0.0)
        totals = jnp.sum(weights, axis=(2, 3)).reshape(per_group * ABLK, 1)
        weights = weights.reshape(per_group * ABLK, key_len).astype(jnp.bfloat16)
        acc = jnp.einsum("qs,cs->qc", weights, v_here[:, :key_len], preferred_element_type=jnp.float32)
        outs.append(acc / totals)
    result = jnp.concatenate(outs, axis=0).astype(jnp.bfloat16)

    back = lax.all_to_all(result.reshape(pieces, ABLK, HD), "seq", 0, 0, tiled=True)
    back = back.reshape(heads, sub, ABLK, HD).transpose(1, 2, 0, 3)
    return back.reshape(rows_dev, channels)


def solution(mesh):
    return jax.shard_map(
        on_device,
        mesh=mesh,
        in_specs=(
            P("seq", "chan"),
            P("seq", "chan"),
            P("seq", "chan"),
            P("chan"),
            P("chan"),
            P("chan", "seq"),
            P("seq", "chan"),
            P("seq", "chan"),
            P("seq", None),
        ),
        out_specs=(P("seq", "chan"), P("seq", "chan")),
        check_vma=False,
    )
```

```python
import math

import numpy as np

import jax
import jax.numpy as jnp
from jax import lax
from jax.sharding import PartitionSpec as P

HD = 128
ABLK = 128

dft_precision = lax.Precision.DEFAULT


def dft_tables(length):
    total = 2 * length
    lanes = 128
    outer = total // lanes
    used = length // lanes
    f32 = lambda a: jnp.asarray(a.astype(np.float32))
    angle_b = 2.0 * np.pi * np.arange(outer)[:, None] * np.arange(used)[None, :] / outer
    angle_a = 2.0 * np.pi * np.arange(lanes)[:, None] * np.arange(lanes)[None, :] / lanes
    angle_t = 2.0 * np.pi * np.arange(outer)[:, None] * np.arange(lanes)[None, :] / total
    return dict(
        cos_b=f32(np.cos(angle_b)),
        sin_b=f32(np.sin(angle_b)),
        cos_a=f32(np.cos(angle_a)),
        sin_a=f32(np.sin(angle_a)),
        cos_t=f32(np.cos(angle_t))[:, None, :],
        sin_t=f32(np.sin(angle_t))[:, None, :],
        inv_cos_b=f32(np.cos(angle_b).T / total),
        inv_sin_b=f32(np.sin(angle_b).T / total),
    )


def mm(spec, a, b):
    return jnp.einsum(spec, a, b, precision=dft_precision, preferred_element_type=jnp.float32)


def forward_dft(data, tab):
    y_re = mm("kn,ncm->kcm", tab["cos_b"], data)
    y_im = -mm("kn,ncm->kcm", tab["sin_b"], data)
    tc, ts = tab["cos_t"], tab["sin_t"]
    t_re = y_re * tc + y_im * ts
    t_im = y_im * tc - y_re * ts
    x_re = mm("kcm,am->kca", t_re, tab["cos_a"]) + mm("kcm,am->kca", t_im, tab["sin_a"])
    x_im = mm("kcm,am->kca", t_im, tab["cos_a"]) - mm("kcm,am->kca", t_re, tab["sin_a"])
    return x_re, x_im


def inverse_dft(p_re, p_im, tab):
    z_re = mm("kca,ta->kct", p_re, tab["cos_a"]) - mm("kca,ta->kct", p_im, tab["sin_a"])
    z_im = mm("kca,ta->kct", p_im, tab["cos_a"]) + mm("kca,ta->kct", p_re, tab["sin_a"])
    tc, ts = tab["cos_t"], tab["sin_t"]
    w_re = z_re * tc - z_im * ts
    w_im = z_re * ts + z_im * tc
    return mm("sk,kct->sct", tab["inv_cos_b"], w_re) - mm("sk,kct->sct", tab["inv_sin_b"], w_im)


def on_device(
    hyena_query, hyena_key, hyena_value, bias, groups, filters, att_queries, att_keys, block_mask
):
    rows_dev, channels = hyena_query.shape
    pieces = lax.axis_size("seq")
    device = lax.axis_index("seq")
    length = rows_dev * pieces
    width = channels // pieces
    tab = dft_tables(length)

    mixed = (hyena_key.astype(jnp.float32) * hyena_value.astype(jnp.float32)).astype(jnp.bfloat16)
    halves = rows_dev // 128
    sends = [
        part.reshape(halves, 128, pieces, width).transpose(2, 0, 3, 1)
        for part in (mixed, hyena_query)
    ]
    got = lax.all_to_all(jnp.concatenate(sends, axis=2), "seq", 0, 0, tiled=True)
    got = got.reshape(pieces * halves, 2 * width, 128)
    mixed_cols = got[:, :width]
    query_cols = got[:, width:]

    chan_count = lax.axis_size("chan")
    local = filters.astype(jnp.bfloat16)
    spread = jnp.broadcast_to(local[None], (chan_count,) + local.shape)
    bank = lax.all_to_all(spread, "chan", 0, 0, tiled=True).reshape(-1, local.shape[1])
    picked = jnp.take(bank, groups.reshape(pieces, width), axis=0)
    picked = picked.reshape(pieces, width, halves, 128).transpose(0, 2, 1, 3)
    kernel = lax.all_to_all(picked, "seq", 0, 0, tiled=True).reshape(pieces * halves, width, 128)

    s_re, s_im = forward_dft(mixed_cols, tab)
    f_re, f_im = forward_dft(kernel, tab)
    conv = inverse_dft(s_re * f_re - s_im * f_im, s_re * f_im + s_im * f_re, tab)
    bias_here = lax.dynamic_slice_in_dim(bias, device * width, width)
    out_cols = (
        query_cols.astype(jnp.float32)
        * (conv + bias_here[None, :, None] * mixed_cols.astype(jnp.float32))
    ).astype(jnp.bfloat16)
    back = lax.all_to_all(out_cols.reshape(pieces, halves, width, 128), "seq", 0, 0, tiled=True)
    hyena_out = back.transpose(1, 3, 0, 2).reshape(rows_dev, channels)
    value_t = out_cols.transpose(1, 0, 2).reshape(width, length)

    attn_out = attention(att_queries, att_keys, value_t, block_mask, pieces, device)
    return (hyena_out, attn_out)


def attention(att_queries, att_keys, value_half, block_mask, pieces, device):
    rows_dev, channels = att_queries.shape
    heads = channels // HD
    length = rows_dev * pieces
    sub = rows_dev // ABLK
    parity = device % sub
    head = device // sub

    block_count = block_mask.shape[1]
    queries = att_queries.reshape(sub, ABLK, heads, HD).transpose(2, 0, 1, 3)
    keys = att_keys.reshape(rows_dev, heads, 1, HD).transpose(1, 2, 0, 3)
    keys = jnp.broadcast_to(keys, (heads, sub, rows_dev, HD))
    mask_pad = jnp.zeros((sub, 8, HD), jnp.bfloat16).at[:, 0, :block_count].set(
        block_mask.astype(jnp.bfloat16)
    )
    mask_pad = jnp.broadcast_to(mask_pad[None], (heads, sub, 8, HD))
    payload = jnp.concatenate([keys, queries, mask_pad], axis=2)
    payload = payload.reshape(heads * sub, rows_dev + ABLK + 8, HD)
    got = lax.all_to_all(payload, "seq", 0, 0, tiled=True)
    k_here = got[:, :rows_dev].reshape(length, HD)
    q_here = got[:, rows_dev : rows_dev + ABLK].reshape(pieces * ABLK, HD)
    mask_rows = got[:, rows_dev + ABLK, :block_count] > 0.5

    pairs = [(source, source ^ 1) for source in range(pieces)]
    other_half = lax.ppermute(value_half, "seq", pairs)
    first = jnp.where(parity == 0, value_half, other_half)
    second = jnp.where(parity == 0, other_half, value_half)
    v_here = jnp.concatenate([first, second], axis=0)

    scale = HD ** (-0.5)
    q_blocks = sub * jnp.arange(pieces, dtype=jnp.int32) + parity
    query_pos = (q_blocks[:, None] * ABLK + jnp.arange(ABLK, dtype=jnp.int32)[None, :]).reshape(-1)
    group_count = 8
    per_group = pieces // group_count
    outs = []
    for g in range(group_count):
        rows = slice(g * per_group * ABLK, (g + 1) * per_group * ABLK)
        key_len = length * (g + 1) // group_count
        kblocks = key_len // ABLK
        block_ok = mask_rows[g * per_group : (g + 1) * per_group, :kblocks]
        q_pos = query_pos[rows].reshape(per_group, ABLK)
        k_pos = jnp.arange(key_len, dtype=jnp.int32).reshape(kblocks, ABLK)
        allowed = block_ok[:, None, :, None] & (
            k_pos[None, None, :, :] <= q_pos[:, :, None, None]
        )
        scores = jnp.dot(q_here[rows], k_here[:key_len].T, preferred_element_type=jnp.float32) * scale
        scores = scores.reshape(per_group, ABLK, kblocks, ABLK)
        scores = jnp.where(allowed, scores, -1e30)
        largest = jnp.max(scores, axis=(2, 3), keepdims=True)
        weights = jnp.where(allowed, jnp.exp(scores - largest), 0.0)
        totals = jnp.sum(weights, axis=(2, 3)).reshape(per_group * ABLK, 1)
        weights = weights.reshape(per_group * ABLK, key_len).astype(jnp.bfloat16)
        acc = jnp.einsum("qs,cs->qc", weights, v_here[:, :key_len], preferred_element_type=jnp.float32)
        outs.append(acc / totals)
    result = jnp.concatenate(outs, axis=0).astype(jnp.bfloat16)

    back = lax.all_to_all(result.reshape(pieces, ABLK, HD), "seq", 0, 0, tiled=True)
    back = back.reshape(heads, sub, ABLK, HD).transpose(1, 2, 0, 3)
    return back.reshape(rows_dev, channels)


def solution(mesh):
    return jax.shard_map(
        on_device,
        mesh=mesh,
        in_specs=(
            P("seq", "chan"),
            P("seq", "chan"),
            P("seq", "chan"),
            P("chan"),
            P("chan"),
            P("chan", "seq"),
            P("seq", "chan"),
            P("seq", "chan"),
            P("seq", None),
        ),
        out_specs=(P("seq", "chan"), P("seq", "chan")),
        check_vma=False,
    )
```

```python
import math

import numpy as np

import jax
import jax.numpy as jnp
from jax import lax
from jax.sharding import PartitionSpec as P

HD = 128
ABLK = 128

dft_precision = lax.Precision.DEFAULT


def dft_tables(length):
    total = 2 * length
    lanes = 128
    outer = total // lanes
    used = length // lanes
    f32 = lambda a: jnp.asarray(a.astype(np.float32))
    angle_b = 2.0 * np.pi * np.arange(outer)[:, None] * np.arange(used)[None, :] / outer
    angle_a = 2.0 * np.pi * np.arange(lanes)[:, None] * np.arange(lanes)[None, :] / lanes
    angle_t = 2.0 * np.pi * np.arange(outer)[:, None] * np.arange(lanes)[None, :] / total
    return dict(
        cos_b=f32(np.cos(angle_b)),
        sin_b=f32(np.sin(angle_b)),
        cos_a=f32(np.cos(angle_a)),
        sin_a=f32(np.sin(angle_a)),
        cos_t=f32(np.cos(angle_t))[:, None, :],
        sin_t=f32(np.sin(angle_t))[:, None, :],
        inv_cos_b=f32(np.cos(angle_b).T / total),
        inv_sin_b=f32(np.sin(angle_b).T / total),
    )


def mm(spec, a, b):
    return jnp.einsum(spec, a, b, precision=dft_precision, preferred_element_type=jnp.float32)


def forward_dft(data, tab):
    y_re = mm("kn,ncm->kcm", tab["cos_b"], data)
    y_im = -mm("kn,ncm->kcm", tab["sin_b"], data)
    tc, ts = tab["cos_t"], tab["sin_t"]
    t_re = y_re * tc + y_im * ts
    t_im = y_im * tc - y_re * ts
    x_re = mm("kcm,am->kca", t_re, tab["cos_a"]) + mm("kcm,am->kca", t_im, tab["sin_a"])
    x_im = mm("kcm,am->kca", t_im, tab["cos_a"]) - mm("kcm,am->kca", t_re, tab["sin_a"])
    return x_re, x_im


def inverse_dft(p_re, p_im, tab):
    z_re = mm("kca,ta->kct", p_re, tab["cos_a"]) - mm("kca,ta->kct", p_im, tab["sin_a"])
    z_im = mm("kca,ta->kct", p_im, tab["cos_a"]) + mm("kca,ta->kct", p_re, tab["sin_a"])
    tc, ts = tab["cos_t"], tab["sin_t"]
    w_re = z_re * tc - z_im * ts
    w_im = z_re * ts + z_im * tc
    return mm("sk,kct->sct", tab["inv_cos_b"], w_re) - mm("sk,kct->sct", tab["inv_sin_b"], w_im)


def on_device(
    hyena_query, hyena_key, hyena_value, bias, groups, filters, att_queries, att_keys, block_mask
):
    rows_dev, channels = hyena_query.shape
    pieces = lax.axis_size("seq")
    device = lax.axis_index("seq")
    length = rows_dev * pieces
    width = channels // pieces
    tab = dft_tables(length)

    got_keys = exchange_keys(att_queries, att_keys, block_mask, pieces)
    mixed = (hyena_key.astype(jnp.float32) * hyena_value.astype(jnp.float32)).astype(jnp.bfloat16)
    halves = rows_dev // 128
    sends = [
        part.reshape(halves, 128, pieces, width).transpose(2, 0, 3, 1)
        for part in (mixed, hyena_query)
    ]
    chan_count = lax.axis_size("chan")
    local = filters.astype(jnp.bfloat16)
    spread = jnp.broadcast_to(local[None], (chan_count,) + local.shape)
    bank = lax.all_to_all(spread, "chan", 0, 0, tiled=True).reshape(-1, local.shape[1])
    picked = jnp.take(bank, groups.reshape(pieces, width), axis=0)
    picked = picked.reshape(pieces, width, halves, 128).transpose(0, 2, 1, 3)
    signal = jnp.concatenate(sends, axis=2)
    got_keys, signal, picked = lax.optimization_barrier((got_keys, signal, picked))

    got = lax.all_to_all(signal, "seq", 0, 0, tiled=True)
    got = got.reshape(pieces * halves, 2 * width, 128)
    mixed_cols = got[:, :width]
    query_cols = got[:, width:]
    kernel = lax.all_to_all(picked, "seq", 0, 0, tiled=True).reshape(pieces * halves, width, 128)

    s_re, s_im = forward_dft(mixed_cols, tab)
    f_re, f_im = forward_dft(kernel, tab)
    conv = inverse_dft(s_re * f_re - s_im * f_im, s_re * f_im + s_im * f_re, tab)
    bias_here = lax.dynamic_slice_in_dim(bias, device * width, width)
    out_cols = (
        query_cols.astype(jnp.float32)
        * (conv + bias_here[None, :, None] * mixed_cols.astype(jnp.float32))
    ).astype(jnp.bfloat16)
    back = lax.all_to_all(out_cols.reshape(pieces, halves, width, 128), "seq", 0, 0, tiled=True)
    hyena_out = back.transpose(1, 3, 0, 2).reshape(rows_dev, channels)
    value_t = out_cols.transpose(1, 0, 2).reshape(width, length)

    attn_out = attention(got_keys, value_t, block_mask, rows_dev, channels, pieces, device)
    return (hyena_out, attn_out)


def exchange_keys(att_queries, att_keys, block_mask, pieces):
    rows_dev, channels = att_queries.shape
    heads = channels // HD
    sub = rows_dev // ABLK
    block_count = block_mask.shape[1]
    queries = att_queries.reshape(sub, ABLK, heads, HD).transpose(2, 0, 1, 3)
    keys = att_keys.reshape(rows_dev, heads, 1, HD).transpose(1, 2, 0, 3)
    keys = jnp.broadcast_to(keys, (heads, sub, rows_dev, HD))
    mask_pad = jnp.zeros((sub, 8, HD), jnp.bfloat16).at[:, 0, :block_count].set(
        block_mask.astype(jnp.bfloat16)
    )
    mask_pad = jnp.broadcast_to(mask_pad[None], (heads, sub, 8, HD))
    payload = jnp.concatenate([keys, queries, mask_pad], axis=2)
    payload = payload.reshape(heads * sub, rows_dev + ABLK + 8, HD)
    return lax.all_to_all(payload, "seq", 0, 0, tiled=True)


def attention(got, value_half, block_mask, rows_dev, channels, pieces, device):
    heads = channels // HD
    length = rows_dev * pieces
    sub = rows_dev // ABLK
    parity = device % sub
    block_count = block_mask.shape[1]
    k_here = got[:, :rows_dev].reshape(length, HD)
    q_here = got[:, rows_dev : rows_dev + ABLK].reshape(pieces * ABLK, HD)
    mask_rows = got[:, rows_dev + ABLK, :block_count] > 0.5

    pairs = [(source, source ^ 1) for source in range(pieces)]
    other_half = lax.ppermute(value_half, "seq", pairs)
    first = jnp.where(parity == 0, value_half, other_half)
    second = jnp.where(parity == 0, other_half, value_half)
    v_here = jnp.concatenate([first, second], axis=0)

    scale = HD ** (-0.5)
    q_blocks = sub * jnp.arange(pieces, dtype=jnp.int32) + parity
    query_pos = (q_blocks[:, None] * ABLK + jnp.arange(ABLK, dtype=jnp.int32)[None, :]).reshape(-1)
    group_count = 8
    per_group = pieces // group_count
    soft = []
    for g in range(group_count):
        rows = slice(g * per_group * ABLK, (g + 1) * per_group * ABLK)
        key_len = length * (g + 1) // group_count
        kblocks = key_len // ABLK
        block_ok = mask_rows[g * per_group : (g + 1) * per_group, :kblocks]
        q_pos = query_pos[rows].reshape(per_group, ABLK)
        k_pos = jnp.arange(key_len, dtype=jnp.int32).reshape(kblocks, ABLK)
        allowed = block_ok[:, None, :, None] & (
            k_pos[None, None, :, :] <= q_pos[:, :, None, None]
        )
        scores = jnp.dot(q_here[rows], k_here[:key_len].T, preferred_element_type=jnp.float32) * scale
        scores = scores.reshape(per_group, ABLK, kblocks, ABLK)
        scores = jnp.where(allowed, scores, -1e30)
        largest = jnp.max(scores, axis=(2, 3), keepdims=True)
        weights = jnp.where(allowed, jnp.exp(scores - largest), 0.0)
        totals = jnp.sum(weights, axis=(2, 3)).reshape(per_group * ABLK, 1)
        weights = weights.reshape(per_group * ABLK, key_len).astype(jnp.bfloat16)
        soft.append((weights, totals))
    soft = lax.optimization_barrier(soft)
    outs = []
    for g, (weights, totals) in enumerate(soft):
        key_len = length * (g + 1) // group_count
        acc = jnp.einsum("qs,cs->qc", weights, v_here[:, :key_len], preferred_element_type=jnp.float32)
        outs.append(acc / totals)
    result = jnp.concatenate(outs, axis=0).astype(jnp.bfloat16)

    back = lax.all_to_all(result.reshape(pieces, ABLK, HD), "seq", 0, 0, tiled=True)
    back = back.reshape(heads, sub, ABLK, HD).transpose(1, 2, 0, 3)
    return back.reshape(rows_dev, channels)


def solution(mesh):
    return jax.shard_map(
        on_device,
        mesh=mesh,
        in_specs=(
            P("seq", "chan"),
            P("seq", "chan"),
            P("seq", "chan"),
            P("chan"),
            P("chan"),
            P("chan", "seq"),
            P("seq", "chan"),
            P("seq", "chan"),
            P("seq", None),
        ),
        out_specs=(P("seq", "chan"), P("seq", "chan")),
        check_vma=False,
    )
```

```python
import math

import numpy as np

import jax
import jax.numpy as jnp
from jax import lax
from jax.sharding import PartitionSpec as P

HD = 128
ABLK = 128

dft_precision = lax.Precision.DEFAULT


def dft_tables(length):
    total = 2 * length
    lanes = 128
    outer = total // lanes
    used = length // lanes
    f32 = lambda a: jnp.asarray(a.astype(np.float32))
    angle_b = 2.0 * np.pi * np.arange(outer)[:, None] * np.arange(used)[None, :] / outer
    angle_a = 2.0 * np.pi * np.arange(lanes)[:, None] * np.arange(lanes)[None, :] / lanes
    angle_t = 2.0 * np.pi * np.arange(outer)[:, None] * np.arange(lanes)[None, :] / total
    return dict(
        cos_b=f32(np.cos(angle_b)),
        sin_b=f32(np.sin(angle_b)),
        cos_a=f32(np.cos(angle_a)),
        sin_a=f32(np.sin(angle_a)),
        cos_t=f32(np.cos(angle_t))[:, None, :],
        sin_t=f32(np.sin(angle_t))[:, None, :],
        inv_cos_b=f32(np.cos(angle_b).T / total),
        inv_sin_b=f32(np.sin(angle_b).T / total),
    )


def mm(spec, a, b):
    return jnp.einsum(spec, a, b, precision=dft_precision, preferred_element_type=jnp.float32)


def forward_dft(data, tab):
    y_re = mm("kn,ncm->kcm", tab["cos_b"], data)
    y_im = -mm("kn,ncm->kcm", tab["sin_b"], data)
    tc, ts = tab["cos_t"], tab["sin_t"]
    t_re = y_re * tc + y_im * ts
    t_im = y_im * tc - y_re * ts
    x_re = mm("kcm,am->kca", t_re, tab["cos_a"]) + mm("kcm,am->kca", t_im, tab["sin_a"])
    x_im = mm("kcm,am->kca", t_im, tab["cos_a"]) - mm("kcm,am->kca", t_re, tab["sin_a"])
    return x_re, x_im


def inverse_dft(p_re, p_im, tab):
    z_re = mm("kca,ta->kct", p_re, tab["cos_a"]) - mm("kca,ta->kct", p_im, tab["sin_a"])
    z_im = mm("kca,ta->kct", p_im, tab["cos_a"]) + mm("kca,ta->kct", p_re, tab["sin_a"])
    tc, ts = tab["cos_t"], tab["sin_t"]
    w_re = z_re * tc - z_im * ts
    w_im = z_re * ts + z_im * tc
    return mm("sk,kct->sct", tab["inv_cos_b"], w_re) - mm("sk,kct->sct", tab["inv_sin_b"], w_im)


def on_device(
    hyena_query, hyena_key, hyena_value, bias, groups, filters, att_queries, att_keys, block_mask
):
    rows_dev, channels = hyena_query.shape
    pieces = lax.axis_size("seq")
    device = lax.axis_index("seq")
    length = rows_dev * pieces
    width = channels // pieces
    tab = dft_tables(length)

    mixed = (hyena_key.astype(jnp.float32) * hyena_value.astype(jnp.float32)).astype(jnp.bfloat16)
    halves = rows_dev // 128
    sends = [
        part.reshape(halves, 128, pieces, width).transpose(2, 0, 3, 1)
        for part in (mixed, hyena_query)
    ]
    chan_count = lax.axis_size("chan")
    local = filters.astype(jnp.bfloat16)
    spread = jnp.broadcast_to(local[None], (chan_count,) + local.shape)
    bank = lax.all_to_all(spread, "chan", 0, 0, tiled=True).reshape(-1, local.shape[1])
    picked = jnp.take(bank, groups.reshape(pieces, width), axis=0)
    picked = picked.reshape(pieces, width, halves, 128).transpose(0, 2, 1, 3)
    sends, picked = lax.optimization_barrier((sends, picked))
    got = lax.all_to_all(jnp.concatenate(sends + [picked], axis=2), "seq", 0, 0, tiled=True)
    got = got.reshape(pieces * halves, 3 * width, 128)
    mixed_cols = got[:, :width]
    query_cols = got[:, width : 2 * width]
    kernel = got[:, 2 * width :]

    s_re, s_im = forward_dft(mixed_cols, tab)
    f_re, f_im = forward_dft(kernel, tab)
    conv = inverse_dft(s_re * f_re - s_im * f_im, s_re * f_im + s_im * f_re, tab)
    bias_here = lax.dynamic_slice_in_dim(bias, device * width, width)
    out_cols = (
        query_cols.astype(jnp.float32)
        * (conv + bias_here[None, :, None] * mixed_cols.astype(jnp.float32))
    ).astype(jnp.bfloat16)
    back = lax.all_to_all(out_cols.reshape(pieces, halves, width, 128), "seq", 0, 0, tiled=True)
    hyena_out = back.transpose(1, 3, 0, 2).reshape(rows_dev, channels)
    value_t = out_cols.transpose(1, 0, 2).reshape(width, length)

    attn_out = attention(att_queries, att_keys, value_t, block_mask, pieces, device)
    return (hyena_out, attn_out)


def attention(att_queries, att_keys, value_half, block_mask, pieces, device):
    rows_dev, channels = att_queries.shape
    heads = channels // HD
    length = rows_dev * pieces
    sub = rows_dev // ABLK
    parity = device % sub
    head = device // sub

    block_count = block_mask.shape[1]
    queries = att_queries.reshape(sub, ABLK, heads, HD).transpose(2, 0, 1, 3)
    keys = att_keys.reshape(rows_dev, heads, 1, HD).transpose(1, 2, 0, 3)
    keys = jnp.broadcast_to(keys, (heads, sub, rows_dev, HD))
    mask_pad = jnp.zeros((sub, 8, HD), jnp.bfloat16).at[:, 0, :block_count].set(
        block_mask.astype(jnp.bfloat16)
    )
    mask_pad = jnp.broadcast_to(mask_pad[None], (heads, sub, 8, HD))
    payload = jnp.concatenate([keys, queries, mask_pad], axis=2)
    payload = payload.reshape(heads * sub, rows_dev + ABLK + 8, HD)
    got = lax.all_to_all(payload, "seq", 0, 0, tiled=True)
    k_here = got[:, :rows_dev].reshape(length, HD)
    q_here = got[:, rows_dev : rows_dev + ABLK].reshape(pieces * ABLK, HD)
    mask_rows = got[:, rows_dev + ABLK, :block_count] > 0.5

    pairs = [(source, source ^ 1) for source in range(pieces)]
    other_half = lax.ppermute(value_half, "seq", pairs)
    first = jnp.where(parity == 0, value_half, other_half)
    second = jnp.where(parity == 0, other_half, value_half)
    v_here = jnp.concatenate([first, second], axis=0)

    scale = HD ** (-0.5)
    q_blocks = sub * jnp.arange(pieces, dtype=jnp.int32) + parity
    query_pos = (q_blocks[:, None] * ABLK + jnp.arange(ABLK, dtype=jnp.int32)[None, :]).reshape(-1)
    group_count = 8
    per_group = pieces // group_count
    outs = []
    for g in range(group_count):
        rows = slice(g * per_group * ABLK, (g + 1) * per_group * ABLK)
        key_len = length * (g + 1) // group_count
        kblocks = key_len // ABLK
        block_ok = mask_rows[g * per_group : (g + 1) * per_group, :kblocks]
        q_pos = query_pos[rows].reshape(per_group, ABLK)
        k_pos = jnp.arange(key_len, dtype=jnp.int32).reshape(kblocks, ABLK)
        allowed = block_ok[:, None, :, None] & (
            k_pos[None, None, :, :] <= q_pos[:, :, None, None]
        )
        scores = jnp.dot(q_here[rows], k_here[:key_len].T, preferred_element_type=jnp.float32) * scale
        scores = scores.reshape(per_group, ABLK, kblocks, ABLK)
        scores = jnp.where(allowed, scores, -1e30)
        largest = jnp.max(scores, axis=(2, 3), keepdims=True)
        weights = jnp.where(allowed, jnp.exp(scores - largest), 0.0)
        totals = jnp.sum(weights, axis=(2, 3)).reshape(per_group * ABLK, 1)
        weights = weights.reshape(per_group * ABLK, key_len).astype(jnp.bfloat16)
        acc = jnp.einsum("qs,cs->qc", weights, v_here[:, :key_len], preferred_element_type=jnp.float32)
        outs.append(acc / totals)
    result = jnp.concatenate(outs, axis=0).astype(jnp.bfloat16)

    back = lax.all_to_all(result.reshape(pieces, ABLK, HD), "seq", 0, 0, tiled=True)
    back = back.reshape(heads, sub, ABLK, HD).transpose(1, 2, 0, 3)
    return back.reshape(rows_dev, channels)


def solution(mesh):
    return jax.shard_map(
        on_device,
        mesh=mesh,
        in_specs=(
            P("seq", "chan"),
            P("seq", "chan"),
            P("seq", "chan"),
            P("chan"),
            P("chan"),
            P("chan", "seq"),
            P("seq", "chan"),
            P("seq", "chan"),
            P("seq", None),
        ),
        out_specs=(P("seq", "chan"), P("seq", "chan")),
        check_vma=False,
    )
```

```python
import math

import numpy as np

import jax
import jax.numpy as jnp
from jax import lax
from jax.sharding import PartitionSpec as P

HD = 128
ABLK = 128

dft_precision = lax.Precision.DEFAULT


def dft_tables(length):
    total = 2 * length
    lanes = 128
    outer = total // lanes
    used = length // lanes
    f32 = lambda a: jnp.asarray(a.astype(np.float32))
    angle_b = 2.0 * np.pi * np.arange(outer)[:, None] * np.arange(used)[None, :] / outer
    angle_a = 2.0 * np.pi * np.arange(lanes)[:, None] * np.arange(lanes)[None, :] / lanes
    angle_t = 2.0 * np.pi * np.arange(outer)[:, None] * np.arange(lanes)[None, :] / total
    return dict(
        cos_b=f32(np.cos(angle_b)),
        sin_b=f32(np.sin(angle_b)),
        cos_a=f32(np.cos(angle_a)),
        sin_a=f32(np.sin(angle_a)),
        cos_t=f32(np.cos(angle_t))[:, None, :],
        sin_t=f32(np.sin(angle_t))[:, None, :],
        inv_cos_b=f32(np.cos(angle_b).T / total),
        inv_sin_b=f32(np.sin(angle_b).T / total),
    )


def mm(spec, a, b):
    return jnp.einsum(spec, a, b, precision=dft_precision, preferred_element_type=jnp.float32)


def forward_dft(data, tab):
    y_re = mm("kn,ncm->kcm", tab["cos_b"], data)
    y_im = -mm("kn,ncm->kcm", tab["sin_b"], data)
    tc, ts = tab["cos_t"], tab["sin_t"]
    t_re = y_re * tc + y_im * ts
    t_im = y_im * tc - y_re * ts
    x_re = mm("kcm,am->kca", t_re, tab["cos_a"]) + mm("kcm,am->kca", t_im, tab["sin_a"])
    x_im = mm("kcm,am->kca", t_im, tab["cos_a"]) - mm("kcm,am->kca", t_re, tab["sin_a"])
    return x_re, x_im


def inverse_dft(p_re, p_im, tab):
    z_re = mm("kca,ta->kct", p_re, tab["cos_a"]) - mm("kca,ta->kct", p_im, tab["sin_a"])
    z_im = mm("kca,ta->kct", p_im, tab["cos_a"]) + mm("kca,ta->kct", p_re, tab["sin_a"])
    tc, ts = tab["cos_t"], tab["sin_t"]
    w_re = z_re * tc - z_im * ts
    w_im = z_re * ts + z_im * tc
    return mm("sk,kct->sct", tab["inv_cos_b"], w_re) - mm("sk,kct->sct", tab["inv_sin_b"], w_im)


def on_device(
    hyena_query, hyena_key, hyena_value, bias, groups, filters, att_queries, att_keys, block_mask
):
    rows_dev, channels = hyena_query.shape
    pieces = lax.axis_size("seq")
    device = lax.axis_index("seq")
    length = rows_dev * pieces
    width = channels // pieces
    tab = dft_tables(length)

    mixed = (hyena_key.astype(jnp.float32) * hyena_value.astype(jnp.float32)).astype(jnp.bfloat16)
    halves = rows_dev // 128
    sends = [
        part.reshape(halves, 128, pieces, width).transpose(2, 0, 3, 1)
        for part in (mixed, hyena_query)
    ]
    chan_count = lax.axis_size("chan")
    local = filters.astype(jnp.bfloat16)
    spread = jnp.broadcast_to(local[None], (chan_count,) + local.shape)
    bank = lax.all_to_all(spread, "chan", 0, 0, tiled=True).reshape(-1, local.shape[1])
    picked = jnp.take(bank, groups.reshape(pieces, width), axis=0)
    picked = picked.reshape(pieces, width, halves, 128).transpose(0, 2, 1, 3)
    sends, picked = lax.optimization_barrier((sends, picked))
    got = lax.all_to_all(jnp.stack(sends + [picked], axis=1), "seq", 0, 0, tiled=True)
    mixed_cols, query_cols, kernel = [
        got[:, part].reshape(pieces * halves, width, 128) for part in range(3)
    ]

    s_re, s_im = forward_dft(mixed_cols, tab)
    f_re, f_im = forward_dft(kernel, tab)
    conv = inverse_dft(s_re * f_re - s_im * f_im, s_re * f_im + s_im * f_re, tab)
    bias_here = lax.dynamic_slice_in_dim(bias, device * width, width)
    out_cols = (
        query_cols.astype(jnp.float32)
        * (conv + bias_here[None, :, None] * mixed_cols.astype(jnp.float32))
    ).astype(jnp.bfloat16)
    back = lax.all_to_all(out_cols.reshape(pieces, halves, width, 128), "seq", 0, 0, tiled=True)
    hyena_out = back.transpose(1, 3, 0, 2).reshape(rows_dev, channels)
    value_t = out_cols.transpose(1, 0, 2).reshape(width, length)

    attn_out = attention(att_queries, att_keys, value_t, block_mask, pieces, device)
    return (hyena_out, attn_out)


def attention(att_queries, att_keys, value_half, block_mask, pieces, device):
    rows_dev, channels = att_queries.shape
    heads = channels // HD
    length = rows_dev * pieces
    sub = rows_dev // ABLK
    parity = device % sub
    head = device // sub

    block_count = block_mask.shape[1]
    queries = att_queries.reshape(sub, ABLK, heads, HD).transpose(2, 0, 1, 3)
    keys = att_keys.reshape(rows_dev, heads, 1, HD).transpose(1, 2, 0, 3)
    keys = jnp.broadcast_to(keys, (heads, sub, rows_dev, HD))
    mask_pad = jnp.zeros((sub, 8, HD), jnp.bfloat16).at[:, 0, :block_count].set(
        block_mask.astype(jnp.bfloat16)
    )
    mask_pad = jnp.broadcast_to(mask_pad[None], (heads, sub, 8, HD))
    payload = jnp.concatenate([keys, queries, mask_pad], axis=2)
    payload = payload.reshape(heads * sub, rows_dev + ABLK + 8, HD)
    got = lax.all_to_all(payload, "seq", 0, 0, tiled=True)
    k_here = got[:, :rows_dev].reshape(length, HD)
    q_here = got[:, rows_dev : rows_dev + ABLK].reshape(pieces * ABLK, HD)
    mask_rows = got[:, rows_dev + ABLK, :block_count] > 0.5

    pairs = [(source, source ^ 1) for source in range(pieces)]
    other_half = lax.ppermute(value_half, "seq", pairs)
    first = jnp.where(parity == 0, value_half, other_half)
    second = jnp.where(parity == 0, other_half, value_half)
    v_here = jnp.concatenate([first, second], axis=0)

    scale = HD ** (-0.5)
    q_blocks = sub * jnp.arange(pieces, dtype=jnp.int32) + parity
    query_pos = (q_blocks[:, None] * ABLK + jnp.arange(ABLK, dtype=jnp.int32)[None, :]).reshape(-1)
    group_count = 8
    per_group = pieces // group_count
    outs = []
    for g in range(group_count):
        rows = slice(g * per_group * ABLK, (g + 1) * per_group * ABLK)
        key_len = length * (g + 1) // group_count
        kblocks = key_len // ABLK
        block_ok = mask_rows[g * per_group : (g + 1) * per_group, :kblocks]
        q_pos = query_pos[rows].reshape(per_group, ABLK)
        k_pos = jnp.arange(key_len, dtype=jnp.int32).reshape(kblocks, ABLK)
        allowed = block_ok[:, None, :, None] & (
            k_pos[None, None, :, :] <= q_pos[:, :, None, None]
        )
        scores = jnp.dot(q_here[rows], k_here[:key_len].T, preferred_element_type=jnp.float32) * scale
        scores = scores.reshape(per_group, ABLK, kblocks, ABLK)
        scores = jnp.where(allowed, scores, -1e30)
        largest = jnp.max(scores, axis=(2, 3), keepdims=True)
        weights = jnp.where(allowed, jnp.exp(scores - largest), 0.0)
        totals = jnp.sum(weights, axis=(2, 3)).reshape(per_group * ABLK, 1)
        weights = weights.reshape(per_group * ABLK, key_len).astype(jnp.bfloat16)
        acc = jnp.einsum("qs,cs->qc", weights, v_here[:, :key_len], preferred_element_type=jnp.float32)
        outs.append(acc / totals)
    result = jnp.concatenate(outs, axis=0).astype(jnp.bfloat16)

    back = lax.all_to_all(result.reshape(pieces, ABLK, HD), "seq", 0, 0, tiled=True)
    back = back.reshape(heads, sub, ABLK, HD).transpose(1, 2, 0, 3)
    return back.reshape(rows_dev, channels)


def solution(mesh):
    return jax.shard_map(
        on_device,
        mesh=mesh,
        in_specs=(
            P("seq", "chan"),
            P("seq", "chan"),
            P("seq", "chan"),
            P("chan"),
            P("chan"),
            P("chan", "seq"),
            P("seq", "chan"),
            P("seq", "chan"),
            P("seq", None),
        ),
        out_specs=(P("seq", "chan"), P("seq", "chan")),
        check_vma=False,
    )
```

```python
import functools

import numpy as np

import jax
import jax.numpy as jnp
from jax import lax
from jax.experimental import pallas as pl
from jax.experimental.pallas import tpu as pltpu
from jax.sharding import PartitionSpec as P

HD = 128
ABLK = 128

dft_precision = lax.Precision.DEFAULT


def dft_tables(length):
    total = 2 * length
    lanes = 128
    outer = total // lanes
    used = length // lanes
    f32 = lambda a: jnp.asarray(a.astype(np.float32))
    angle_b = 2.0 * np.pi * np.arange(outer)[:, None] * np.arange(used)[None, :] / outer
    angle_a = 2.0 * np.pi * np.arange(lanes)[:, None] * np.arange(lanes)[None, :] / lanes
    angle_t = 2.0 * np.pi * np.arange(outer)[:, None] * np.arange(lanes)[None, :] / total
    return dict(
        cos_b=f32(np.cos(angle_b)),
        sin_b=f32(np.sin(angle_b)),
        cos_a=f32(np.cos(angle_a)),
        sin_a=f32(np.sin(angle_a)),
        cos_t=f32(np.cos(angle_t))[:, None, :],
        sin_t=f32(np.sin(angle_t))[:, None, :],
        inv_cos_b=f32(np.cos(angle_b).T / total),
        inv_sin_b=f32(np.sin(angle_b).T / total),
    )


def mm(spec, a, b):
    return jnp.einsum(spec, a, b, precision=dft_precision, preferred_element_type=jnp.float32)


def forward_dft(data, tab):
    y_re = mm("kn,ncm->kcm", tab["cos_b"], data)
    y_im = -mm("kn,ncm->kcm", tab["sin_b"], data)
    tc, ts = tab["cos_t"], tab["sin_t"]
    t_re = y_re * tc + y_im * ts
    t_im = y_im * tc - y_re * ts
    x_re = mm("kcm,am->kca", t_re, tab["cos_a"]) + mm("kcm,am->kca", t_im, tab["sin_a"])
    x_im = mm("kcm,am->kca", t_im, tab["cos_a"]) - mm("kcm,am->kca", t_re, tab["sin_a"])
    return x_re, x_im


def inverse_dft(p_re, p_im, tab):
    z_re = mm("kca,ta->kct", p_re, tab["cos_a"]) - mm("kca,ta->kct", p_im, tab["sin_a"])
    z_im = mm("kca,ta->kct", p_im, tab["cos_a"]) + mm("kca,ta->kct", p_re, tab["sin_a"])
    tc, ts = tab["cos_t"], tab["sin_t"]
    w_re = z_re * tc - z_im * ts
    w_im = z_re * ts + z_im * tc
    return mm("sk,kct->sct", tab["inv_cos_b"], w_re) - mm("sk,kct->sct", tab["inv_sin_b"], w_im)


def on_device(
    hyena_query, hyena_key, hyena_value, bias, groups, filters, att_queries, att_keys, block_mask
):
    rows_dev, channels = hyena_query.shape
    pieces = lax.axis_size("seq")
    device = lax.axis_index("seq")
    length = rows_dev * pieces
    width = channels // pieces
    tab = dft_tables(length)

    mixed = (hyena_key.astype(jnp.float32) * hyena_value.astype(jnp.float32)).astype(jnp.bfloat16)
    halves = rows_dev // 128
    sends = [
        part.reshape(halves, 128, pieces, width).transpose(2, 0, 3, 1)
        for part in (mixed, hyena_query)
    ]
    chan_count = lax.axis_size("chan")
    local = filters.astype(jnp.bfloat16)
    spread = jnp.broadcast_to(local[None], (chan_count,) + local.shape)
    bank = lax.all_to_all(spread, "chan", 0, 0, tiled=True).reshape(-1, local.shape[1])
    picked = jnp.take(bank, groups.reshape(pieces, width), axis=0)
    picked = picked.reshape(pieces, width, halves, 128).transpose(0, 2, 1, 3)
    sends, picked = lax.optimization_barrier((sends, picked))
    got = lax.all_to_all(jnp.stack(sends + [picked], axis=1), "seq", 0, 0, tiled=True)
    mixed_cols, query_cols, kernel = [
        got[:, part].reshape(pieces * halves, width, 128) for part in range(3)
    ]

    s_re, s_im = forward_dft(mixed_cols, tab)
    f_re, f_im = forward_dft(kernel, tab)
    conv = inverse_dft(s_re * f_re - s_im * f_im, s_re * f_im + s_im * f_re, tab)
    bias_here = lax.dynamic_slice_in_dim(bias, device * width, width)
    out_cols = (
        query_cols.astype(jnp.float32)
        * (conv + bias_here[None, :, None] * mixed_cols.astype(jnp.float32))
    ).astype(jnp.bfloat16)
    back = lax.all_to_all(out_cols.reshape(pieces, halves, width, 128), "seq", 0, 0, tiled=True)
    hyena_out = back.transpose(1, 3, 0, 2).reshape(rows_dev, channels)
    value_t = out_cols.transpose(1, 0, 2).reshape(width, length)

    attn_out = attention(att_queries, att_keys, value_t, block_mask, pieces, device)
    return (hyena_out, attn_out)


def flash_body(mask_ref, par_ref, q_ref, k_ref, vt_ref, o_ref, m_sc, l_sc, acc_sc, *, sub, scale):
    r = pl.program_id(0)
    b = sub * r + par_ref[0]
    q = q_ref[...]
    m_sc[...] = jnp.full(m_sc.shape, -1e30, jnp.float32)
    l_sc[...] = jnp.zeros(l_sc.shape, jnp.float32)
    acc_sc[...] = jnp.zeros(acc_sc.shape, jnp.float32)

    def body(kb, carry):
        @pl.when(mask_ref[r, kb] == 1)
        def _():
            start = pl.multiple_of(kb * ABLK, ABLK)
            kblk = k_ref[pl.ds(start, ABLK), :]
            s = lax.dot_general(q, kblk, (((1,), (1,)), ((), ())), preferred_element_type=jnp.float32)
            s = s * scale
            row = lax.broadcasted_iota(jnp.int32, s.shape, 0) + b * ABLK
            col = lax.broadcasted_iota(jnp.int32, s.shape, 1) + start
            s = jnp.where(col <= row, s, -1e30)
            m_old = m_sc[...]
            m_new = jnp.maximum(m_old, jnp.max(s, axis=1, keepdims=True))
            alpha = jnp.exp(m_old - m_new)
            p = jnp.exp(s - m_new)
            l_sc[...] = alpha * l_sc[...] + jnp.sum(p, axis=1, keepdims=True)
            vblk = vt_ref[:, pl.ds(start, ABLK)]
            pv = lax.dot_general(
                p.astype(jnp.bfloat16), vblk, (((1,), (1,)), ((), ())), preferred_element_type=jnp.float32
            )
            acc_sc[...] = alpha * acc_sc[...] + pv
            m_sc[...] = m_new

        return carry

    lax.fori_loop(0, b + 1, body, 0)
    o_ref[...] = (acc_sc[...] / l_sc[...]).astype(o_ref.dtype)


def flash(mask_rows, parity, q, k, vt, sub):
    tiles = q.shape[0] // ABLK
    length = k.shape[0]
    grid_spec = pltpu.PrefetchScalarGridSpec(
        num_scalar_prefetch=2,
        grid=(tiles,),
        in_specs=[
            pl.BlockSpec((ABLK, HD), lambda r, m, p: (r, 0)),
            pl.BlockSpec((length, HD), lambda r, m, p: (0, 0)),
            pl.BlockSpec((HD, length), lambda r, m, p: (0, 0)),
        ],
        out_specs=pl.BlockSpec((ABLK, HD), lambda r, m, p: (r, 0)),
        scratch_shapes=[
            pltpu.VMEM((ABLK, 1), jnp.float32),
            pltpu.VMEM((ABLK, 1), jnp.float32),
            pltpu.VMEM((ABLK, HD), jnp.float32),
        ],
    )
    return pl.pallas_call(
        functools.partial(flash_body, sub=sub, scale=HD ** (-0.5)),
        grid_spec=grid_spec,
        out_shape=jax.ShapeDtypeStruct((tiles * ABLK, HD), jnp.bfloat16),
        compiler_params=pltpu.CompilerParams(dimension_semantics=("arbitrary",)),
    )(mask_rows, parity, q, k, vt)


def attention(att_queries, att_keys, value_half, block_mask, pieces, device):
    rows_dev, channels = att_queries.shape
    heads = channels // HD
    length = rows_dev * pieces
    sub = rows_dev // ABLK
    parity = device % sub
    head = device // sub

    block_count = block_mask.shape[1]
    queries = att_queries.reshape(sub, ABLK, heads, HD).transpose(2, 0, 1, 3)
    keys = att_keys.reshape(rows_dev, heads, 1, HD).transpose(1, 2, 0, 3)
    keys = jnp.broadcast_to(keys, (heads, sub, rows_dev, HD))
    mask_pad = jnp.zeros((sub, 8, HD), jnp.bfloat16).at[:, 0, :block_count].set(
        block_mask.astype(jnp.bfloat16)
    )
    mask_pad = jnp.broadcast_to(mask_pad[None], (heads, sub, 8, HD))
    payload = jnp.concatenate([keys, queries, mask_pad], axis=2)
    payload = payload.reshape(heads * sub, rows_dev + ABLK + 8, HD)
    got = lax.all_to_all(payload, "seq", 0, 0, tiled=True)
    k_here = got[:, :rows_dev].reshape(length, HD)
    q_here = got[:, rows_dev : rows_dev + ABLK].reshape(pieces * ABLK, HD)
    mask_rows = got[:, rows_dev + ABLK, :block_count] > 0.5

    pairs = [(source, source ^ 1) for source in range(pieces)]
    other_half = lax.ppermute(value_half, "seq", pairs)
    first = jnp.where(parity == 0, value_half, other_half)
    second = jnp.where(parity == 0, other_half, value_half)
    v_here = jnp.concatenate([first, second], axis=0)

    parity_arr = jnp.reshape(parity, (1,)).astype(jnp.int32)
    result = flash(mask_rows.astype(jnp.int32), parity_arr, q_here, k_here, v_here, sub)

    back = lax.all_to_all(result.reshape(pieces, ABLK, HD), "seq", 0, 0, tiled=True)
    back = back.reshape(heads, sub, ABLK, HD).transpose(1, 2, 0, 3)
    return back.reshape(rows_dev, channels)


def solution(mesh):
    return jax.shard_map(
        on_device,
        mesh=mesh,
        in_specs=(
            P("seq", "chan"),
            P("seq", "chan"),
            P("seq", "chan"),
            P("chan"),
            P("chan"),
            P("chan", "seq"),
            P("seq", "chan"),
            P("seq", "chan"),
            P("seq", None),
        ),
        out_specs=(P("seq", "chan"), P("seq", "chan")),
        check_vma=False,
    )
```

```python
import math

import numpy as np

import jax
import jax.numpy as jnp
from jax import lax
from jax.sharding import PartitionSpec as P

HD = 128
ABLK = 128

dft_precision = lax.Precision.DEFAULT


def dft_tables(length):
    total = 2 * length
    lanes = 128
    outer = total // lanes
    used = length // lanes
    f32 = lambda a: jnp.asarray(a.astype(np.float32))
    angle_b = 2.0 * np.pi * np.arange(outer)[:, None] * np.arange(used)[None, :] / outer
    angle_a = 2.0 * np.pi * np.arange(lanes)[:, None] * np.arange(lanes)[None, :] / lanes
    angle_t = 2.0 * np.pi * np.arange(outer)[:, None] * np.arange(lanes)[None, :] / total
    return dict(
        cos_b=f32(np.cos(angle_b)),
        sin_b=f32(np.sin(angle_b)),
        cos_a=f32(np.cos(angle_a)),
        sin_a=f32(np.sin(angle_a)),
        cos_t=f32(np.cos(angle_t))[:, None, :],
        sin_t=f32(np.sin(angle_t))[:, None, :],
        inv_cos_b=f32(np.cos(angle_b).T / total),
        inv_sin_b=f32(np.sin(angle_b).T / total),
    )


def mm(spec, a, b):
    return jnp.einsum(spec, a, b, precision=dft_precision, preferred_element_type=jnp.float32)


def forward_dft(data, tab):
    y_re = mm("kn,ncm->kcm", tab["cos_b"], data)
    y_im = -mm("kn,ncm->kcm", tab["sin_b"], data)
    tc, ts = tab["cos_t"], tab["sin_t"]
    t_re = y_re * tc + y_im * ts
    t_im = y_im * tc - y_re * ts
    x_re = mm("kcm,am->kca", t_re, tab["cos_a"]) + mm("kcm,am->kca", t_im, tab["sin_a"])
    x_im = mm("kcm,am->kca", t_im, tab["cos_a"]) - mm("kcm,am->kca", t_re, tab["sin_a"])
    return x_re, x_im


def inverse_dft(p_re, p_im, tab):
    z_re = mm("kca,ta->kct", p_re, tab["cos_a"]) - mm("kca,ta->kct", p_im, tab["sin_a"])
    z_im = mm("kca,ta->kct", p_im, tab["cos_a"]) + mm("kca,ta->kct", p_re, tab["sin_a"])
    tc, ts = tab["cos_t"], tab["sin_t"]
    w_re = z_re * tc - z_im * ts
    w_im = z_re * ts + z_im * tc
    return mm("sk,kct->sct", tab["inv_cos_b"], w_re) - mm("sk,kct->sct", tab["inv_sin_b"], w_im)


def on_device(
    hyena_query, hyena_key, hyena_value, bias, groups, filters, att_queries, att_keys, block_mask
):
    rows_dev, channels = hyena_query.shape
    pieces = lax.axis_size("seq")
    device = lax.axis_index("seq")
    length = rows_dev * pieces
    width = channels // pieces
    tab = dft_tables(length)

    mixed = (hyena_key.astype(jnp.float32) * hyena_value.astype(jnp.float32)).astype(jnp.bfloat16)
    halves = rows_dev // 128
    sends = [
        part.reshape(halves, 128, pieces, width).transpose(2, 0, 3, 1)
        for part in (mixed, hyena_query)
    ]
    chan_count = lax.axis_size("chan")
    local = filters.astype(jnp.bfloat16)
    spread = jnp.broadcast_to(local[None], (chan_count,) + local.shape)
    bank = lax.all_to_all(spread, "chan", 0, 0, tiled=True).reshape(-1, local.shape[1])
    picked = jnp.take(bank, groups.reshape(pieces, width), axis=0)
    picked = picked.reshape(pieces, width, halves, 128).transpose(0, 2, 1, 3)
    sends, picked = lax.optimization_barrier((sends, picked))
    stacked = jnp.stack([sends[0], picked, sends[1]], axis=2)
    got = lax.all_to_all(stacked, "seq", 0, 0, tiled=True).reshape(pieces * halves, 3 * width, 128)
    both = got[:, : 2 * width]
    mixed_cols = got[:, :width]
    query_cols = got[:, 2 * width :]

    b_re, b_im = forward_dft(both, tab)
    s_re, f_re = b_re[:, :width], b_re[:, width:]
    s_im, f_im = b_im[:, :width], b_im[:, width:]
    conv = inverse_dft(s_re * f_re - s_im * f_im, s_re * f_im + s_im * f_re, tab)
    bias_here = lax.dynamic_slice_in_dim(bias, device * width, width)
    out_cols = (
        query_cols.astype(jnp.float32)
        * (conv + bias_here[None, :, None] * mixed_cols.astype(jnp.float32))
    ).astype(jnp.bfloat16)
    back = lax.all_to_all(out_cols.reshape(pieces, halves, width, 128), "seq", 0, 0, tiled=True)
    hyena_out = back.transpose(1, 3, 0, 2).reshape(rows_dev, channels)
    value_t = out_cols.transpose(1, 0, 2).reshape(width, length)

    attn_out = attention(att_queries, att_keys, value_t, block_mask, pieces, device)
    return (hyena_out, attn_out)


def attention(att_queries, att_keys, value_half, block_mask, pieces, device):
    rows_dev, channels = att_queries.shape
    heads = channels // HD
    length = rows_dev * pieces
    sub = rows_dev // ABLK
    parity = device % sub
    head = device // sub

    block_count = block_mask.shape[1]
    queries = att_queries.reshape(sub, ABLK, heads, HD).transpose(2, 0, 1, 3)
    keys = att_keys.reshape(rows_dev, heads, 1, HD).transpose(1, 2, 0, 3)
    keys = jnp.broadcast_to(keys, (heads, sub, rows_dev, HD))
    mask_pad = jnp.zeros((sub, 8, HD), jnp.bfloat16).at[:, 0, :block_count].set(
        block_mask.astype(jnp.bfloat16)
    )
    mask_pad = jnp.broadcast_to(mask_pad[None], (heads, sub, 8, HD))
    payload = jnp.concatenate([keys, queries, mask_pad], axis=2)
    payload = payload.reshape(heads * sub, rows_dev + ABLK + 8, HD)
    got = lax.all_to_all(payload, "seq", 0, 0, tiled=True)
    k_here = got[:, :rows_dev].reshape(length, HD)
    q_here = got[:, rows_dev : rows_dev + ABLK].reshape(pieces * ABLK, HD)
    mask_rows = got[:, rows_dev + ABLK, :block_count] > 0.5

    pairs = [(source, source ^ 1) for source in range(pieces)]
    other_half = lax.ppermute(value_half, "seq", pairs)
    first = jnp.where(parity == 0, value_half, other_half)
    second = jnp.where(parity == 0, other_half, value_half)
    v_here = jnp.concatenate([first, second], axis=0)

    scale = HD ** (-0.5)
    q_blocks = sub * jnp.arange(pieces, dtype=jnp.int32) + parity
    query_pos = (q_blocks[:, None] * ABLK + jnp.arange(ABLK, dtype=jnp.int32)[None, :]).reshape(-1)
    group_count = 8
    per_group = pieces // group_count
    outs = []
    for g in range(group_count):
        rows = slice(g * per_group * ABLK, (g + 1) * per_group * ABLK)
        key_len = length * (g + 1) // group_count
        kblocks = key_len // ABLK
        block_ok = mask_rows[g * per_group : (g + 1) * per_group, :kblocks]
        q_pos = query_pos[rows].reshape(per_group, ABLK)
        k_pos = jnp.arange(key_len, dtype=jnp.int32).reshape(kblocks, ABLK)
        allowed = block_ok[:, None, :, None] & (
            k_pos[None, None, :, :] <= q_pos[:, :, None, None]
        )
        scores = jnp.dot(q_here[rows], k_here[:key_len].T, preferred_element_type=jnp.float32) * scale
        scores = scores.reshape(per_group, ABLK, kblocks, ABLK)
        scores = jnp.where(allowed, scores, -1e30)
        largest = jnp.max(scores, axis=(2, 3), keepdims=True)
        weights = jnp.where(allowed, jnp.exp(scores - largest), 0.0)
        totals = jnp.sum(weights, axis=(2, 3)).reshape(per_group * ABLK, 1)
        weights = weights.reshape(per_group * ABLK, key_len).astype(jnp.bfloat16)
        acc = jnp.einsum("qs,cs->qc", weights, v_here[:, :key_len], preferred_element_type=jnp.float32)
        outs.append(acc / totals)
    result = jnp.concatenate(outs, axis=0).astype(jnp.bfloat16)

    back = lax.all_to_all(result.reshape(pieces, ABLK, HD), "seq", 0, 0, tiled=True)
    back = back.reshape(heads, sub, ABLK, HD).transpose(1, 2, 0, 3)
    return back.reshape(rows_dev, channels)


def solution(mesh):
    return jax.shard_map(
        on_device,
        mesh=mesh,
        in_specs=(
            P("seq", "chan"),
            P("seq", "chan"),
            P("seq", "chan"),
            P("chan"),
            P("chan"),
            P("chan", "seq"),
            P("seq", "chan"),
            P("seq", "chan"),
            P("seq", None),
        ),
        out_specs=(P("seq", "chan"), P("seq", "chan")),
        check_vma=False,
    )
```

```python
import math

import numpy as np

import jax
import jax.numpy as jnp
from jax import lax
from jax.sharding import PartitionSpec as P

HD = 128
ABLK = 128

dft_precision = lax.Precision.DEFAULT


def dft_tables(length):
    total = 2 * length
    lanes = 128
    outer = total // lanes
    used = length // lanes
    f32 = lambda a: jnp.asarray(a.astype(np.float32))
    angle_b = 2.0 * np.pi * np.arange(outer)[:, None] * np.arange(used)[None, :] / outer
    angle_a = 2.0 * np.pi * np.arange(lanes)[:, None] * np.arange(lanes)[None, :] / lanes
    angle_t = 2.0 * np.pi * np.arange(outer)[:, None] * np.arange(lanes)[None, :] / total
    return dict(
        cos_b=f32(np.cos(angle_b)),
        sin_b=f32(np.sin(angle_b)),
        cos_a=f32(np.cos(angle_a)),
        sin_a=f32(np.sin(angle_a)),
        cos_t=f32(np.cos(angle_t))[:, None, :],
        sin_t=f32(np.sin(angle_t))[:, None, :],
        inv_cos_b=f32(np.cos(angle_b).T / total),
        inv_sin_b=f32(np.sin(angle_b).T / total),
    )


def mm(spec, a, b):
    return jnp.einsum(spec, a, b, precision=dft_precision, preferred_element_type=jnp.float32)


def forward_dft(data, tab):
    y_re = mm("kn,ncm->kcm", tab["cos_b"], data)
    y_im = -mm("kn,ncm->kcm", tab["sin_b"], data)
    tc, ts = tab["cos_t"], tab["sin_t"]
    t_re = y_re * tc + y_im * ts
    t_im = y_im * tc - y_re * ts
    x_re = mm("kcm,am->kca", t_re, tab["cos_a"]) + mm("kcm,am->kca", t_im, tab["sin_a"])
    x_im = mm("kcm,am->kca", t_im, tab["cos_a"]) - mm("kcm,am->kca", t_re, tab["sin_a"])
    return x_re, x_im


def inverse_dft(p_re, p_im, tab):
    z_re = mm("kca,ta->kct", p_re, tab["cos_a"]) - mm("kca,ta->kct", p_im, tab["sin_a"])
    z_im = mm("kca,ta->kct", p_im, tab["cos_a"]) + mm("kca,ta->kct", p_re, tab["sin_a"])
    tc, ts = tab["cos_t"], tab["sin_t"]
    w_re = z_re * tc - z_im * ts
    w_im = z_re * ts + z_im * tc
    return mm("sk,kct->sct", tab["inv_cos_b"], w_re) - mm("sk,kct->sct", tab["inv_sin_b"], w_im)


def on_device(
    hyena_query, hyena_key, hyena_value, bias, groups, filters, att_queries, att_keys, block_mask
):
    rows_dev, channels = hyena_query.shape
    pieces = lax.axis_size("seq")
    device = lax.axis_index("seq")
    length = rows_dev * pieces
    width = channels // pieces
    tab = dft_tables(length)

    mixed = (hyena_key.astype(jnp.float32) * hyena_value.astype(jnp.float32)).astype(jnp.bfloat16)
    halves = rows_dev // 128
    sends = [
        part.reshape(halves, 128, pieces, width).transpose(2, 0, 3, 1)
        for part in (mixed, hyena_query)
    ]
    chan_count = lax.axis_size("chan")
    local = filters.astype(jnp.bfloat16)
    shifted = [local] + [
        lax.ppermute(local, "chan", [(c, (c + k) % chan_count) for c in range(chan_count)])
        for k in range(1, chan_count)
    ]
    bank = jnp.concatenate(shifted, axis=0)
    chan_here = lax.axis_index("chan")
    per_chan = local.shape[0]
    home = groups // per_chan
    row = ((chan_here - home) % chan_count) * per_chan + groups % per_chan
    picked = jnp.take(bank, row.reshape(pieces, width), axis=0)
    picked = picked.reshape(pieces, width, halves, 128).transpose(0, 2, 1, 3)
    sends, picked = lax.optimization_barrier((sends, picked))
    stacked = jnp.stack([sends[0], picked, sends[1]], axis=2)
    got = lax.all_to_all(stacked, "seq", 0, 0, tiled=True).reshape(pieces * halves, 3 * width, 128)
    both = got[:, : 2 * width]
    mixed_cols = got[:, :width]
    query_cols = got[:, 2 * width :]

    b_re, b_im = forward_dft(both, tab)
    s_re, f_re = b_re[:, :width], b_re[:, width:]
    s_im, f_im = b_im[:, :width], b_im[:, width:]
    conv = inverse_dft(s_re * f_re - s_im * f_im, s_re * f_im + s_im * f_re, tab)
    bias_here = lax.dynamic_slice_in_dim(bias, device * width, width)
    out_cols = (
        query_cols.astype(jnp.float32)
        * (conv + bias_here[None, :, None] * mixed_cols.astype(jnp.float32))
    ).astype(jnp.bfloat16)
    back = lax.all_to_all(out_cols.reshape(pieces, halves, width, 128), "seq", 0, 0, tiled=True)
    hyena_out = back.transpose(1, 3, 0, 2).reshape(rows_dev, channels)
    value_t = out_cols.transpose(1, 0, 2).reshape(width, length)

    attn_out = attention(att_queries, att_keys, value_t, block_mask, pieces, device)
    return (hyena_out, attn_out)


def attention(att_queries, att_keys, value_half, block_mask, pieces, device):
    rows_dev, channels = att_queries.shape
    heads = channels // HD
    length = rows_dev * pieces
    sub = rows_dev // ABLK
    parity = device % sub
    head = device // sub

    block_count = block_mask.shape[1]
    queries = att_queries.reshape(sub, ABLK, heads, HD).transpose(2, 0, 1, 3)
    keys = att_keys.reshape(rows_dev, heads, 1, HD).transpose(1, 2, 0, 3)
    keys = jnp.broadcast_to(keys, (heads, sub, rows_dev, HD))
    mask_pad = jnp.zeros((sub, 8, HD), jnp.bfloat16).at[:, 0, :block_count].set(
        block_mask.astype(jnp.bfloat16)
    )
    mask_pad = jnp.broadcast_to(mask_pad[None], (heads, sub, 8, HD))
    payload = jnp.concatenate([keys, queries, mask_pad], axis=2)
    payload = payload.reshape(heads * sub, rows_dev + ABLK + 8, HD)
    got = lax.all_to_all(payload, "seq", 0, 0, tiled=True)
    k_here = got[:, :rows_dev].reshape(length, HD)
    q_here = got[:, rows_dev : rows_dev + ABLK].reshape(pieces * ABLK, HD)
    mask_rows = got[:, rows_dev + ABLK, :block_count] > 0.5

    pairs = [(source, source ^ 1) for source in range(pieces)]
    other_half = lax.ppermute(value_half, "seq", pairs)
    first = jnp.where(parity == 0, value_half, other_half)
    second = jnp.where(parity == 0, other_half, value_half)
    v_here = jnp.concatenate([first, second], axis=0)

    scale = HD ** (-0.5)
    q_blocks = sub * jnp.arange(pieces, dtype=jnp.int32) + parity
    query_pos = (q_blocks[:, None] * ABLK + jnp.arange(ABLK, dtype=jnp.int32)[None, :]).reshape(-1)
    group_count = 8
    per_group = pieces // group_count
    outs = []
    for g in range(group_count):
        rows = slice(g * per_group * ABLK, (g + 1) * per_group * ABLK)
        key_len = length * (g + 1) // group_count
        kblocks = key_len // ABLK
        block_ok = mask_rows[g * per_group : (g + 1) * per_group, :kblocks]
        q_pos = query_pos[rows].reshape(per_group, ABLK)
        k_pos = jnp.arange(key_len, dtype=jnp.int32).reshape(kblocks, ABLK)
        allowed = block_ok[:, None, :, None] & (
            k_pos[None, None, :, :] <= q_pos[:, :, None, None]
        )
        scores = jnp.dot(q_here[rows], k_here[:key_len].T, preferred_element_type=jnp.float32) * scale
        scores = scores.reshape(per_group, ABLK, kblocks, ABLK)
        scores = jnp.where(allowed, scores, -1e30)
        largest = jnp.max(scores, axis=(2, 3), keepdims=True)
        weights = jnp.where(allowed, jnp.exp(scores - largest), 0.0)
        totals = jnp.sum(weights, axis=(2, 3)).reshape(per_group * ABLK, 1)
        weights = weights.reshape(per_group * ABLK, key_len).astype(jnp.bfloat16)
        acc = jnp.einsum("qs,cs->qc", weights, v_here[:, :key_len], preferred_element_type=jnp.float32)
        outs.append(acc / totals)
    result = jnp.concatenate(outs, axis=0).astype(jnp.bfloat16)

    back = lax.all_to_all(result.reshape(pieces, ABLK, HD), "seq", 0, 0, tiled=True)
    back = back.reshape(heads, sub, ABLK, HD).transpose(1, 2, 0, 3)
    return back.reshape(rows_dev, channels)


def solution(mesh):
    return jax.shard_map(
        on_device,
        mesh=mesh,
        in_specs=(
            P("seq", "chan"),
            P("seq", "chan"),
            P("seq", "chan"),
            P("chan"),
            P("chan"),
            P("chan", "seq"),
            P("seq", "chan"),
            P("seq", "chan"),
            P("seq", None),
        ),
        out_specs=(P("seq", "chan"), P("seq", "chan")),
        check_vma=False,
    )
```

```python
import math

import numpy as np

import jax
import jax.numpy as jnp
from jax import lax
from jax.sharding import PartitionSpec as P

HD = 128
ABLK = 128

dft_precision = lax.Precision.DEFAULT


def dft_tables(length):
    total = 2 * length
    lanes = 128
    outer = total // lanes
    used = length // lanes
    f32 = lambda a: jnp.asarray(a.astype(np.float32))
    angle_b = 2.0 * np.pi * np.arange(outer)[:, None] * np.arange(used)[None, :] / outer
    angle_a = 2.0 * np.pi * np.arange(lanes)[:, None] * np.arange(lanes)[None, :] / lanes
    angle_t = 2.0 * np.pi * np.arange(outer)[:, None] * np.arange(lanes)[None, :] / total
    return dict(
        cos_b=f32(np.cos(angle_b)),
        sin_b=f32(np.sin(angle_b)),
        cos_a=f32(np.cos(angle_a)),
        sin_a=f32(np.sin(angle_a)),
        cos_t=f32(np.cos(angle_t))[:, None, :],
        sin_t=f32(np.sin(angle_t))[:, None, :],
        inv_cos_b=f32(np.cos(angle_b).T / total),
        inv_sin_b=f32(np.sin(angle_b).T / total),
    )


def mm(spec, a, b):
    return jnp.einsum(spec, a, b, precision=dft_precision, preferred_element_type=jnp.float32)


def forward_dft(data, tab):
    y_re = mm("kn,ncm->kcm", tab["cos_b"], data)
    y_im = -mm("kn,ncm->kcm", tab["sin_b"], data)
    tc, ts = tab["cos_t"], tab["sin_t"]
    t_re = y_re * tc + y_im * ts
    t_im = y_im * tc - y_re * ts
    x_re = mm("kcm,am->kca", t_re, tab["cos_a"]) + mm("kcm,am->kca", t_im, tab["sin_a"])
    x_im = mm("kcm,am->kca", t_im, tab["cos_a"]) - mm("kcm,am->kca", t_re, tab["sin_a"])
    return x_re, x_im


def inverse_dft(p_re, p_im, tab):
    z_re = mm("kca,ta->kct", p_re, tab["cos_a"]) - mm("kca,ta->kct", p_im, tab["sin_a"])
    z_im = mm("kca,ta->kct", p_im, tab["cos_a"]) + mm("kca,ta->kct", p_re, tab["sin_a"])
    tc, ts = tab["cos_t"], tab["sin_t"]
    w_re = z_re * tc - z_im * ts
    w_im = z_re * ts + z_im * tc
    return mm("sk,kct->sct", tab["inv_cos_b"], w_re) - mm("sk,kct->sct", tab["inv_sin_b"], w_im)


def on_device(
    hyena_query, hyena_key, hyena_value, bias, groups, filters, att_queries, att_keys, block_mask
):
    rows_dev, channels = hyena_query.shape
    pieces = lax.axis_size("seq")
    device = lax.axis_index("seq")
    length = rows_dev * pieces
    width = channels // pieces
    tab = dft_tables(length)

    mixed = (hyena_key.astype(jnp.float32) * hyena_value.astype(jnp.float32)).astype(jnp.bfloat16)
    halves = rows_dev // 128
    sends = [
        part.reshape(halves, 128, pieces, width).transpose(2, 0, 3, 1)
        for part in (mixed, hyena_query)
    ]
    chan_count = lax.axis_size("chan")
    local = filters.astype(jnp.bfloat16)
    spread = jnp.broadcast_to(local[None], (chan_count,) + local.shape)
    bank = lax.all_to_all(spread, "chan", 0, 0, tiled=True).reshape(-1, local.shape[1])
    picked = jnp.take(bank, groups.reshape(pieces, width), axis=0)
    picked = picked.reshape(pieces, width, halves, 128).transpose(0, 2, 1, 3)
    sends, picked = lax.optimization_barrier((sends, picked))
    stacked = jnp.stack([sends[0], picked, sends[1]], axis=2)
    got = lax.all_to_all(stacked, "seq", 0, 0, tiled=True).reshape(pieces * halves, 3 * width, 128)
    both = got[:, : 2 * width]
    mixed_cols = got[:, :width]
    query_cols = got[:, 2 * width :]

    b_re, b_im = forward_dft(both, tab)
    s_re, f_re = b_re[:, :width], b_re[:, width:]
    s_im, f_im = b_im[:, :width], b_im[:, width:]
    conv = inverse_dft(s_re * f_re - s_im * f_im, s_re * f_im + s_im * f_re, tab)
    bias_here = lax.dynamic_slice_in_dim(bias, device * width, width)
    out_cols = (
        query_cols.astype(jnp.float32)
        * (conv + bias_here[None, :, None] * mixed_cols.astype(jnp.float32))
    ).astype(jnp.bfloat16)
    back = lax.all_to_all(out_cols.reshape(pieces, halves, width, 128), "seq", 0, 0, tiled=True)
    hyena_out = back.transpose(1, 3, 0, 2).reshape(rows_dev, channels)
    value_t = out_cols.transpose(1, 0, 2).reshape(width, length)

    attn_out = attention(att_queries, att_keys, value_t, block_mask, pieces, device)
    return (hyena_out, attn_out)


def attention(att_queries, att_keys, value_half, block_mask, pieces, device):
    rows_dev, channels = att_queries.shape
    heads = channels // HD
    length = rows_dev * pieces
    sub = rows_dev // ABLK
    parity = device % sub
    head = device // sub

    block_count = block_mask.shape[1]
    queries = att_queries.reshape(sub, ABLK, heads, HD).transpose(2, 0, 1, 3)
    keys = att_keys.reshape(sub, ABLK, heads, HD).transpose(2, 0, 1, 3)
    mask_pad = jnp.zeros((sub, 8, HD), jnp.bfloat16).at[:, 0, :block_count].set(
        block_mask.astype(jnp.bfloat16)
    )
    mask_pad = jnp.broadcast_to(mask_pad[None], (heads, sub, 8, HD))
    payload = jnp.concatenate([keys, queries, mask_pad], axis=2)
    payload = payload.reshape(heads * sub, 2 * ABLK + 8, HD)
    got = lax.all_to_all(payload, "seq", 0, 0, tiled=True)
    pairs = [(source, source ^ 1) for source in range(pieces)]
    k_own = got[:, :ABLK]
    k_other = lax.ppermute(k_own, "seq", pairs)
    k_low = jnp.where(parity == 0, k_own, k_other)
    k_high = jnp.where(parity == 0, k_other, k_own)
    k_here = jnp.stack([k_low, k_high], axis=1).reshape(length, HD)
    q_here = got[:, ABLK : 2 * ABLK].reshape(pieces * ABLK, HD)
    mask_rows = got[:, 2 * ABLK, :block_count] > 0.5

    other_half = lax.ppermute(value_half, "seq", pairs)
    first = jnp.where(parity == 0, value_half, other_half)
    second = jnp.where(parity == 0, other_half, value_half)
    v_here = jnp.concatenate([first, second], axis=0)

    scale = HD ** (-0.5)
    q_blocks = sub * jnp.arange(pieces, dtype=jnp.int32) + parity
    query_pos = (q_blocks[:, None] * ABLK + jnp.arange(ABLK, dtype=jnp.int32)[None, :]).reshape(-1)
    group_count = 8
    per_group = pieces // group_count
    outs = []
    for g in range(group_count):
        rows = slice(g * per_group * ABLK, (g + 1) * per_group * ABLK)
        key_len = length * (g + 1) // group_count
        kblocks = key_len // ABLK
        block_ok = mask_rows[g * per_group : (g + 1) * per_group, :kblocks]
        q_pos = query_pos[rows].reshape(per_group, ABLK)
        k_pos = jnp.arange(key_len, dtype=jnp.int32).reshape(kblocks, ABLK)
        allowed = block_ok[:, None, :, None] & (
            k_pos[None, None, :, :] <= q_pos[:, :, None, None]
        )
        scores = jnp.dot(q_here[rows], k_here[:key_len].T, preferred_element_type=jnp.float32) * scale
        scores = scores.reshape(per_group, ABLK, kblocks, ABLK)
        scores = jnp.where(allowed, scores, -1e30)
        largest = jnp.max(scores, axis=(2, 3), keepdims=True)
        weights = jnp.where(allowed, jnp.exp(scores - largest), 0.0)
        totals = jnp.sum(weights, axis=(2, 3)).reshape(per_group * ABLK, 1)
        weights = weights.reshape(per_group * ABLK, key_len).astype(jnp.bfloat16)
        acc = jnp.einsum("qs,cs->qc", weights, v_here[:, :key_len], preferred_element_type=jnp.float32)
        outs.append(acc / totals)
    result = jnp.concatenate(outs, axis=0).astype(jnp.bfloat16)

    back = lax.all_to_all(result.reshape(pieces, ABLK, HD), "seq", 0, 0, tiled=True)
    back = back.reshape(heads, sub, ABLK, HD).transpose(1, 2, 0, 3)
    return back.reshape(rows_dev, channels)


def solution(mesh):
    return jax.shard_map(
        on_device,
        mesh=mesh,
        in_specs=(
            P("seq", "chan"),
            P("seq", "chan"),
            P("seq", "chan"),
            P("chan"),
            P("chan"),
            P("chan", "seq"),
            P("seq", "chan"),
            P("seq", "chan"),
            P("seq", None),
        ),
        out_specs=(P("seq", "chan"), P("seq", "chan")),
        check_vma=False,
    )
```

```python
import math

import numpy as np

import jax
import jax.numpy as jnp
from jax import lax
from jax.sharding import PartitionSpec as P

HD = 128
ABLK = 128

dft_precision = lax.Precision.DEFAULT


def dft_tables(length):
    total = 2 * length
    lanes = 128
    outer = total // lanes
    used = length // lanes
    f32 = lambda a: jnp.asarray(a.astype(np.float32))
    angle_b = 2.0 * np.pi * np.arange(outer)[:, None] * np.arange(used)[None, :] / outer
    angle_a = 2.0 * np.pi * np.arange(lanes)[:, None] * np.arange(lanes)[None, :] / lanes
    angle_t = 2.0 * np.pi * np.arange(outer)[:, None] * np.arange(lanes)[None, :] / total
    return dict(
        cos_b=f32(np.cos(angle_b)),
        sin_b=f32(np.sin(angle_b)),
        cos_a=f32(np.cos(angle_a)),
        sin_a=f32(np.sin(angle_a)),
        cos_t=f32(np.cos(angle_t))[:, None, :],
        sin_t=f32(np.sin(angle_t))[:, None, :],
        inv_cos_b=f32(np.cos(angle_b).T / total),
        inv_sin_b=f32(np.sin(angle_b).T / total),
    )


def mm(spec, a, b):
    return jnp.einsum(spec, a, b, precision=dft_precision, preferred_element_type=jnp.float32)


def forward_dft(data, tab):
    y_re = mm("kn,ncm->kcm", tab["cos_b"], data)
    y_im = -mm("kn,ncm->kcm", tab["sin_b"], data)
    tc, ts = tab["cos_t"], tab["sin_t"]
    t_re = y_re * tc + y_im * ts
    t_im = y_im * tc - y_re * ts
    x_re = mm("kcm,am->kca", t_re, tab["cos_a"]) + mm("kcm,am->kca", t_im, tab["sin_a"])
    x_im = mm("kcm,am->kca", t_im, tab["cos_a"]) - mm("kcm,am->kca", t_re, tab["sin_a"])
    return x_re, x_im


def inverse_dft(p_re, p_im, tab):
    z_re = mm("kca,ta->kct", p_re, tab["cos_a"]) - mm("kca,ta->kct", p_im, tab["sin_a"])
    z_im = mm("kca,ta->kct", p_im, tab["cos_a"]) + mm("kca,ta->kct", p_re, tab["sin_a"])
    tc, ts = tab["cos_t"], tab["sin_t"]
    w_re = z_re * tc - z_im * ts
    w_im = z_re * ts + z_im * tc
    return mm("sk,kct->sct", tab["inv_cos_b"], w_re) - mm("sk,kct->sct", tab["inv_sin_b"], w_im)


def on_device(
    hyena_query, hyena_key, hyena_value, bias, groups, filters, att_queries, att_keys, block_mask
):
    rows_dev, channels = hyena_query.shape
    pieces = lax.axis_size("seq")
    device = lax.axis_index("seq")
    length = rows_dev * pieces
    width = channels // pieces
    tab = dft_tables(length)

    mixed = (hyena_key.astype(jnp.float32) * hyena_value.astype(jnp.float32)).astype(jnp.bfloat16)
    halves = rows_dev // 128
    sends = [
        part.reshape(halves, 128, pieces, width).transpose(2, 0, 3, 1)
        for part in (mixed, hyena_query)
    ]
    chan_count = lax.axis_size("chan")
    local = filters.astype(jnp.bfloat16)
    spread = jnp.broadcast_to(local[None], (chan_count,) + local.shape)
    bank = lax.all_to_all(spread, "chan", 0, 0, tiled=True).reshape(-1, local.shape[1])
    picked = jnp.take(bank, groups.reshape(pieces, width), axis=0)
    picked = picked.reshape(pieces, width, halves, 128).transpose(0, 2, 1, 3)
    sends, picked = lax.optimization_barrier((sends, picked))
    stacked = jnp.stack([sends[0], picked, sends[1]], axis=2)
    got = lax.all_to_all(stacked, "seq", 0, 0, tiled=True).reshape(pieces * halves, 3 * width, 128)
    both = got[:, : 2 * width]
    mixed_cols = got[:, :width]
    query_cols = got[:, 2 * width :]

    b_re, b_im = forward_dft(both, tab)
    s_re, f_re = b_re[:, :width], b_re[:, width:]
    s_im, f_im = b_im[:, :width], b_im[:, width:]
    conv = inverse_dft(s_re * f_re - s_im * f_im, s_re * f_im + s_im * f_re, tab)
    bias_here = lax.dynamic_slice_in_dim(bias, device * width, width)
    out_cols = (
        query_cols.astype(jnp.float32)
        * (conv + bias_here[None, :, None] * mixed_cols.astype(jnp.float32))
    ).astype(jnp.bfloat16)
    back = lax.all_to_all(out_cols.reshape(pieces, halves, width, 128), "seq", 0, 0, tiled=True)
    hyena_out = back.transpose(1, 3, 0, 2).reshape(rows_dev, channels)
    value_t = out_cols.transpose(1, 0, 2).reshape(width, length)

    attn_out = attention(att_queries, att_keys, value_t, block_mask, pieces, device, got)
    return (hyena_out, attn_out)


def attention(att_queries, att_keys, value_half, block_mask, pieces, device, arrived):
    rows_dev, channels = att_queries.shape
    heads = channels // HD
    length = rows_dev * pieces
    sub = rows_dev // ABLK
    parity = device % sub
    head = device // sub

    block_count = block_mask.shape[1]
    queries = att_queries.reshape(sub, ABLK, heads, HD).transpose(2, 0, 1, 3)
    keys = att_keys.reshape(sub, ABLK, heads, HD).transpose(2, 0, 1, 3)
    mask_pad = jnp.zeros((sub, 8, HD), jnp.bfloat16).at[:, 0, :block_count].set(
        block_mask.astype(jnp.bfloat16)
    )
    mask_pad = jnp.broadcast_to(mask_pad[None], (heads, sub, 8, HD))
    payload = jnp.concatenate([keys, queries, mask_pad], axis=2)
    payload = payload.reshape(heads * sub, 2 * ABLK + 8, HD)
    got = lax.all_to_all(payload, "seq", 0, 0, tiled=True)
    pairs = [(source, source ^ 1) for source in range(pieces)]
    k_own, _ = lax.optimization_barrier((got[:, :ABLK], arrived))
    k_other = lax.ppermute(k_own, "seq", pairs)
    k_low = jnp.where(parity == 0, k_own, k_other)
    k_high = jnp.where(parity == 0, k_other, k_own)
    k_here = jnp.stack([k_low, k_high], axis=1).reshape(length, HD)
    q_here = got[:, ABLK : 2 * ABLK].reshape(pieces * ABLK, HD)
    mask_rows = got[:, 2 * ABLK, :block_count] > 0.5
    k_here, q_here, value_half = lax.optimization_barrier((k_here, q_here, value_half))

    other_half = lax.ppermute(value_half, "seq", pairs)
    first = jnp.where(parity == 0, value_half, other_half)
    second = jnp.where(parity == 0, other_half, value_half)
    v_here = jnp.concatenate([first, second], axis=0)

    scale = HD ** (-0.5)
    q_blocks = sub * jnp.arange(pieces, dtype=jnp.int32) + parity
    query_pos = (q_blocks[:, None] * ABLK + jnp.arange(ABLK, dtype=jnp.int32)[None, :]).reshape(-1)
    group_count = 8
    per_group = pieces // group_count
    outs = []
    for g in range(group_count):
        rows = slice(g * per_group * ABLK, (g + 1) * per_group * ABLK)
        key_len = length * (g + 1) // group_count
        kblocks = key_len // ABLK
        block_ok = mask_rows[g * per_group : (g + 1) * per_group, :kblocks]
        q_pos = query_pos[rows].reshape(per_group, ABLK)
        k_pos = jnp.arange(key_len, dtype=jnp.int32).reshape(kblocks, ABLK)
        allowed = block_ok[:, None, :, None] & (
            k_pos[None, None, :, :] <= q_pos[:, :, None, None]
        )
        scores = jnp.dot(q_here[rows], k_here[:key_len].T, preferred_element_type=jnp.float32) * scale
        scores = scores.reshape(per_group, ABLK, kblocks, ABLK)
        scores = jnp.where(allowed, scores, -1e30)
        largest = jnp.max(scores, axis=(2, 3), keepdims=True)
        weights = jnp.where(allowed, jnp.exp(scores - largest), 0.0)
        totals = jnp.sum(weights, axis=(2, 3)).reshape(per_group * ABLK, 1)
        weights = weights.reshape(per_group * ABLK, key_len).astype(jnp.bfloat16)
        acc = jnp.einsum("qs,cs->qc", weights, v_here[:, :key_len], preferred_element_type=jnp.float32)
        outs.append(acc / totals)
    result = jnp.concatenate(outs, axis=0).astype(jnp.bfloat16)

    back = lax.all_to_all(result.reshape(pieces, ABLK, HD), "seq", 0, 0, tiled=True)
    back = back.reshape(heads, sub, ABLK, HD).transpose(1, 2, 0, 3)
    return back.reshape(rows_dev, channels)


def solution(mesh):
    return jax.shard_map(
        on_device,
        mesh=mesh,
        in_specs=(
            P("seq", "chan"),
            P("seq", "chan"),
            P("seq", "chan"),
            P("chan"),
            P("chan"),
            P("chan", "seq"),
            P("seq", "chan"),
            P("seq", "chan"),
            P("seq", None),
        ),
        out_specs=(P("seq", "chan"), P("seq", "chan")),
        check_vma=False,
    )
```

```python
import math

import numpy as np

import jax
import jax.numpy as jnp
from jax import lax
from jax.sharding import PartitionSpec as P

HD = 128
ABLK = 128

dft_precision = lax.Precision.DEFAULT


def dft_tables(length):
    total = 2 * length
    lanes = 128
    outer = total // lanes
    used = length // lanes
    f32 = lambda a: jnp.asarray(a.astype(np.float32))
    angle_b = 2.0 * np.pi * np.arange(outer)[:, None] * np.arange(used)[None, :] / outer
    angle_a = 2.0 * np.pi * np.arange(lanes)[:, None] * np.arange(lanes)[None, :] / lanes
    angle_t = 2.0 * np.pi * np.arange(outer)[:, None] * np.arange(lanes)[None, :] / total
    return dict(
        cos_b=f32(np.cos(angle_b)),
        sin_b=f32(np.sin(angle_b)),
        cos_a=f32(np.cos(angle_a)),
        sin_a=f32(np.sin(angle_a)),
        cos_t=f32(np.cos(angle_t))[:, None, :],
        sin_t=f32(np.sin(angle_t))[:, None, :],
        inv_cos_b=f32(np.cos(angle_b).T / total),
        inv_sin_b=f32(np.sin(angle_b).T / total),
    )


def mm(spec, a, b):
    return jnp.einsum(spec, a, b, precision=dft_precision, preferred_element_type=jnp.float32)


def forward_dft(data, tab):
    y_re = mm("kn,ncm->kcm", tab["cos_b"], data)
    y_im = -mm("kn,ncm->kcm", tab["sin_b"], data)
    tc, ts = tab["cos_t"], tab["sin_t"]
    t_re = y_re * tc + y_im * ts
    t_im = y_im * tc - y_re * ts
    x_re = mm("kcm,am->kca", t_re, tab["cos_a"]) + mm("kcm,am->kca", t_im, tab["sin_a"])
    x_im = mm("kcm,am->kca", t_im, tab["cos_a"]) - mm("kcm,am->kca", t_re, tab["sin_a"])
    return x_re, x_im


def inverse_dft(p_re, p_im, tab):
    z_re = mm("kca,ta->kct", p_re, tab["cos_a"]) - mm("kca,ta->kct", p_im, tab["sin_a"])
    z_im = mm("kca,ta->kct", p_im, tab["cos_a"]) + mm("kca,ta->kct", p_re, tab["sin_a"])
    tc, ts = tab["cos_t"], tab["sin_t"]
    w_re = z_re * tc - z_im * ts
    w_im = z_re * ts + z_im * tc
    return mm("sk,kct->sct", tab["inv_cos_b"], w_re) - mm("sk,kct->sct", tab["inv_sin_b"], w_im)


def on_device(
    hyena_query, hyena_key, hyena_value, bias, groups, filters, att_queries, att_keys, block_mask
):
    rows_dev, channels = hyena_query.shape
    pieces = lax.axis_size("seq")
    device = lax.axis_index("seq")
    length = rows_dev * pieces
    width = channels // pieces
    tab = dft_tables(length)

    mixed = (hyena_key.astype(jnp.float32) * hyena_value.astype(jnp.float32)).astype(jnp.bfloat16)
    halves = rows_dev // 128
    sends = [
        part.reshape(halves, 128, pieces, width).transpose(2, 0, 3, 1)
        for part in (mixed, hyena_query)
    ]
    chan_count = lax.axis_size("chan")
    local = filters.astype(jnp.bfloat16)
    spread = jnp.broadcast_to(local[None], (chan_count,) + local.shape)
    bank = lax.all_to_all(spread, "chan", 0, 0, tiled=True).reshape(-1, local.shape[1])
    picked = jnp.take(bank, groups.reshape(pieces, width), axis=0)
    picked = picked.reshape(pieces, width, halves, 128).transpose(0, 2, 1, 3)
    sends, picked = lax.optimization_barrier((sends, picked))
    stacked = jnp.stack([sends[0], picked, sends[1]], axis=2)
    got = lax.all_to_all(stacked, "seq", 0, 0, tiled=True).reshape(pieces * halves, 3 * width, 128)
    both = got[:, : 2 * width]
    mixed_cols = got[:, :width]
    query_cols = got[:, 2 * width :]

    b_re, b_im = forward_dft(both, tab)
    s_re, f_re = b_re[:, :width], b_re[:, width:]
    s_im, f_im = b_im[:, :width], b_im[:, width:]
    conv = inverse_dft(s_re * f_re - s_im * f_im, s_re * f_im + s_im * f_re, tab)
    bias_here = lax.dynamic_slice_in_dim(bias, device * width, width)
    out_cols = (
        query_cols.astype(jnp.float32)
        * (conv + bias_here[None, :, None] * mixed_cols.astype(jnp.float32))
    ).astype(jnp.bfloat16)
    back = lax.all_to_all(out_cols.reshape(pieces, halves, width, 128), "seq", 0, 0, tiled=True)
    hyena_out = back.transpose(1, 3, 0, 2).reshape(rows_dev, channels)
    value_t = out_cols.transpose(1, 0, 2).reshape(width, length)

    attn_out = attention(att_queries, att_keys, value_t, block_mask, pieces, device, got)
    return (hyena_out, attn_out)


def attention(att_queries, att_keys, value_half, block_mask, pieces, device, arrived):
    rows_dev, channels = att_queries.shape
    heads = channels // HD
    length = rows_dev * pieces
    sub = rows_dev // ABLK
    parity = device % sub
    head = device // sub

    block_count = block_mask.shape[1]
    queries = att_queries.reshape(sub, ABLK, heads, HD).transpose(2, 0, 1, 3)
    keys = att_keys.reshape(rows_dev, heads, 1, HD).transpose(1, 2, 0, 3)
    keys = jnp.broadcast_to(keys, (heads, sub, rows_dev, HD))
    mask_pad = jnp.zeros((sub, 8, HD), jnp.bfloat16).at[:, 0, :block_count].set(
        block_mask.astype(jnp.bfloat16)
    )
    mask_pad = jnp.broadcast_to(mask_pad[None], (heads, sub, 8, HD))
    payload = jnp.concatenate([keys, queries, mask_pad], axis=2)
    payload = payload.reshape(heads * sub, rows_dev + ABLK + 8, HD)
    payload, _ = lax.optimization_barrier((payload, arrived))
    got = lax.all_to_all(payload, "seq", 0, 0, tiled=True)
    k_here = got[:, :rows_dev].reshape(length, HD)
    q_here = got[:, rows_dev : rows_dev + ABLK].reshape(pieces * ABLK, HD)
    mask_rows = got[:, rows_dev + ABLK, :block_count] > 0.5

    pairs = [(source, source ^ 1) for source in range(pieces)]
    other_half = lax.ppermute(value_half, "seq", pairs)
    first = jnp.where(parity == 0, value_half, other_half)
    second = jnp.where(parity == 0, other_half, value_half)
    v_here = jnp.concatenate([first, second], axis=0)

    scale = HD ** (-0.5)
    q_blocks = sub * jnp.arange(pieces, dtype=jnp.int32) + parity
    query_pos = (q_blocks[:, None] * ABLK + jnp.arange(ABLK, dtype=jnp.int32)[None, :]).reshape(-1)
    group_count = 8
    per_group = pieces // group_count
    outs = []
    for g in range(group_count):
        rows = slice(g * per_group * ABLK, (g + 1) * per_group * ABLK)
        key_len = length * (g + 1) // group_count
        kblocks = key_len // ABLK
        block_ok = mask_rows[g * per_group : (g + 1) * per_group, :kblocks]
        q_pos = query_pos[rows].reshape(per_group, ABLK)
        k_pos = jnp.arange(key_len, dtype=jnp.int32).reshape(kblocks, ABLK)
        allowed = block_ok[:, None, :, None] & (
            k_pos[None, None, :, :] <= q_pos[:, :, None, None]
        )
        scores = jnp.dot(q_here[rows], k_here[:key_len].T, preferred_element_type=jnp.float32) * scale
        scores = scores.reshape(per_group, ABLK, kblocks, ABLK)
        scores = jnp.where(allowed, scores, -1e30)
        largest = jnp.max(scores, axis=(2, 3), keepdims=True)
        weights = jnp.where(allowed, jnp.exp(scores - largest), 0.0)
        totals = jnp.sum(weights, axis=(2, 3)).reshape(per_group * ABLK, 1)
        weights = weights.reshape(per_group * ABLK, key_len).astype(jnp.bfloat16)
        acc = jnp.einsum("qs,cs->qc", weights, v_here[:, :key_len], preferred_element_type=jnp.float32)
        outs.append(acc / totals)
    result = jnp.concatenate(outs, axis=0).astype(jnp.bfloat16)

    back = lax.all_to_all(result.reshape(pieces, ABLK, HD), "seq", 0, 0, tiled=True)
    back = back.reshape(heads, sub, ABLK, HD).transpose(1, 2, 0, 3)
    return back.reshape(rows_dev, channels)


def solution(mesh):
    return jax.shard_map(
        on_device,
        mesh=mesh,
        in_specs=(
            P("seq", "chan"),
            P("seq", "chan"),
            P("seq", "chan"),
            P("chan"),
            P("chan"),
            P("chan", "seq"),
            P("seq", "chan"),
            P("seq", "chan"),
            P("seq", None),
        ),
        out_specs=(P("seq", "chan"), P("seq", "chan")),
        check_vma=False,
    )
```

```python
import math

import numpy as np

import jax
import jax.numpy as jnp
from jax import lax
from jax.sharding import PartitionSpec as P

HD = 128
ABLK = 128

dft_precision = lax.Precision.DEFAULT


def dft_tables(length):
    total = 2 * length
    lanes = 128
    outer = total // lanes
    used = length // lanes
    f32 = lambda a: jnp.asarray(a.astype(np.float32))
    angle_b = 2.0 * np.pi * np.arange(outer)[:, None] * np.arange(used)[None, :] / outer
    angle_a = 2.0 * np.pi * np.arange(lanes)[:, None] * np.arange(lanes)[None, :] / lanes
    angle_t = 2.0 * np.pi * np.arange(outer)[:, None] * np.arange(lanes)[None, :] / total
    return dict(
        cos_b=f32(np.cos(angle_b)),
        sin_b=f32(np.sin(angle_b)),
        cos_a=f32(np.cos(angle_a)),
        sin_a=f32(np.sin(angle_a)),
        cos_t=f32(np.cos(angle_t))[:, None, :],
        sin_t=f32(np.sin(angle_t))[:, None, :],
        inv_cos_b=f32(np.cos(angle_b).T / total),
        inv_sin_b=f32(np.sin(angle_b).T / total),
    )


def mm(spec, a, b):
    return jnp.einsum(spec, a, b, precision=dft_precision, preferred_element_type=jnp.float32)


def forward_dft(data, tab):
    y_re = mm("kn,ncm->kcm", tab["cos_b"], data)
    y_im = -mm("kn,ncm->kcm", tab["sin_b"], data)
    tc, ts = tab["cos_t"], tab["sin_t"]
    t_re = y_re * tc + y_im * ts
    t_im = y_im * tc - y_re * ts
    x_re = mm("kcm,am->kca", t_re, tab["cos_a"]) + mm("kcm,am->kca", t_im, tab["sin_a"])
    x_im = mm("kcm,am->kca", t_im, tab["cos_a"]) - mm("kcm,am->kca", t_re, tab["sin_a"])
    return x_re, x_im


def inverse_dft(p_re, p_im, tab):
    z_re = mm("kca,ta->kct", p_re, tab["cos_a"]) - mm("kca,ta->kct", p_im, tab["sin_a"])
    z_im = mm("kca,ta->kct", p_im, tab["cos_a"]) + mm("kca,ta->kct", p_re, tab["sin_a"])
    tc, ts = tab["cos_t"], tab["sin_t"]
    w_re = z_re * tc - z_im * ts
    w_im = z_re * ts + z_im * tc
    return mm("sk,kct->sct", tab["inv_cos_b"], w_re) - mm("sk,kct->sct", tab["inv_sin_b"], w_im)


def on_device(
    hyena_query, hyena_key, hyena_value, bias, groups, filters, att_queries, att_keys, block_mask
):
    rows_dev, channels = hyena_query.shape
    pieces = lax.axis_size("seq")
    device = lax.axis_index("seq")
    length = rows_dev * pieces
    width = channels // pieces
    tab = dft_tables(length)

    mixed = (hyena_key.astype(jnp.float32) * hyena_value.astype(jnp.float32)).astype(jnp.bfloat16)
    halves = rows_dev // 128
    sends = [
        part.reshape(halves, 128, pieces, width).transpose(2, 0, 3, 1)
        for part in (mixed, hyena_query)
    ]
    got = lax.all_to_all(jnp.concatenate(sends, axis=2), "seq", 0, 0, tiled=True)
    got = got.reshape(pieces * halves, 2 * width, 128)
    mixed_cols = got[:, :width]
    query_cols = got[:, width:]

    chan_count = lax.axis_size("chan")
    local = filters.astype(jnp.bfloat16)
    spread = jnp.broadcast_to(local[None], (chan_count,) + local.shape)
    bank = lax.all_to_all(spread, "chan", 0, 0, tiled=True).reshape(-1, local.shape[1])
    picked = jnp.take(bank, groups.reshape(pieces, width), axis=0)
    picked = picked.reshape(pieces, width, halves, 128).transpose(0, 2, 1, 3)
    kernel = lax.all_to_all(picked, "seq", 0, 0, tiled=True).reshape(pieces * halves, width, 128)

    s_re, s_im = forward_dft(mixed_cols, tab)
    f_re, f_im = forward_dft(kernel, tab)
    conv = inverse_dft(s_re * f_re - s_im * f_im, s_re * f_im + s_im * f_re, tab)
    bias_here = lax.dynamic_slice_in_dim(bias, device * width, width)
    out_cols = (
        query_cols.astype(jnp.float32)
        * (conv + bias_here[None, :, None] * mixed_cols.astype(jnp.float32))
    ).astype(jnp.bfloat16)
    back = lax.all_to_all(out_cols.reshape(pieces, halves, width, 128), "seq", 0, 0, tiled=True)
    hyena_out = back.transpose(1, 3, 0, 2).reshape(rows_dev, channels)
    value_t = out_cols.transpose(1, 0, 2).reshape(width, length)

    attn_out = attention(att_queries, att_keys, value_t, block_mask, pieces, device)
    return (hyena_out, attn_out)


def attention(att_queries, att_keys, value_half, block_mask, pieces, device):
    rows_dev, channels = att_queries.shape
    heads = channels // HD
    length = rows_dev * pieces
    sub = rows_dev // ABLK
    parity = device % sub
    head = device // sub

    block_count = block_mask.shape[1]
    queries = att_queries.reshape(sub, ABLK, heads, HD).transpose(2, 0, 1, 3)
    keys = att_keys.reshape(rows_dev, heads, 1, HD).transpose(1, 2, 0, 3)
    keys = jnp.broadcast_to(keys, (heads, sub, rows_dev, HD))
    mask_pad = jnp.zeros((sub, 8, HD), jnp.bfloat16).at[:, 0, :block_count].set(
        block_mask.astype(jnp.bfloat16)
    )
    mask_pad = jnp.broadcast_to(mask_pad[None], (heads, sub, 8, HD))
    payload = jnp.concatenate([keys, queries, mask_pad], axis=2)
    payload = payload.reshape(heads * sub, rows_dev + ABLK + 8, HD)
    got = lax.all_to_all(payload, "seq", 0, 0, tiled=True)
    k_here = got[:, :rows_dev].reshape(length, HD)
    q_here = got[:, rows_dev : rows_dev + ABLK].reshape(pieces * ABLK, HD)
    mask_rows = got[:, rows_dev + ABLK, :block_count] > 0.5

    pairs = [(source, source ^ 1) for source in range(pieces)]
    other_half = lax.ppermute(value_half, "seq", pairs)
    first = jnp.where(parity == 0, value_half, other_half)
    second = jnp.where(parity == 0, other_half, value_half)
    v_here = jnp.concatenate([first, second], axis=0)

    scale = HD ** (-0.5)
    q_blocks = sub * jnp.arange(pieces, dtype=jnp.int32) + parity
    query_pos = (q_blocks[:, None] * ABLK + jnp.arange(ABLK, dtype=jnp.int32)[None, :]).reshape(-1)
    group_count = 4
    per_group = pieces // group_count
    outs = []
    for g in range(group_count):
        rows = slice(g * per_group * ABLK, (g + 1) * per_group * ABLK)
        key_len = length * (g + 1) // group_count
        kblocks = key_len // ABLK
        block_ok = mask_rows[g * per_group : (g + 1) * per_group, :kblocks]
        q_pos = query_pos[rows].reshape(per_group, ABLK)
        k_pos = jnp.arange(key_len, dtype=jnp.int32).reshape(kblocks, ABLK)
        allowed = block_ok[:, None, :, None] & (
            k_pos[None, None, :, :] <= q_pos[:, :, None, None]
        )
        scores = jnp.dot(q_here[rows], k_here[:key_len].T, preferred_element_type=jnp.float32) * scale
        scores = scores.reshape(per_group, ABLK, kblocks, ABLK)
        scores = jnp.where(allowed, scores, -1e30)
        largest = jnp.max(scores, axis=(2, 3), keepdims=True)
        weights = jnp.exp(scores - largest)
        totals = jnp.sum(weights, axis=(2, 3)).reshape(per_group * ABLK, 1)
        weights = weights.reshape(per_group * ABLK, key_len).astype(jnp.bfloat16)
        acc = jnp.einsum("qs,cs->qc", weights, v_here[:, :key_len], preferred_element_type=jnp.float32)
        outs.append(acc / totals)
    result = jnp.concatenate(outs, axis=0).astype(jnp.bfloat16)

    back = lax.all_to_all(result.reshape(pieces, ABLK, HD), "seq", 0, 0, tiled=True)
    back = back.reshape(heads, sub, ABLK, HD).transpose(1, 2, 0, 3)
    return back.reshape(rows_dev, channels)


def solution(mesh):
    return jax.shard_map(
        on_device,
        mesh=mesh,
        in_specs=(
            P("seq", "chan"),
            P("seq", "chan"),
            P("seq", "chan"),
            P("chan"),
            P("chan"),
            P("chan", "seq"),
            P("seq", "chan"),
            P("seq", "chan"),
            P("seq", None),
        ),
        out_specs=(P("seq", "chan"), P("seq", "chan")),
        check_vma=False,
    )
```

```python
import math

import numpy as np

import jax
import jax.numpy as jnp
from jax import lax
from jax.sharding import PartitionSpec as P

HD = 128
ABLK = 128

dft_precision = lax.Precision.DEFAULT


def dft_tables(length):
    total = 2 * length
    lanes = 128
    outer = total // lanes
    used = length // lanes
    f32 = lambda a: jnp.asarray(a.astype(np.float32))
    angle_b = 2.0 * np.pi * np.arange(outer)[:, None] * np.arange(used)[None, :] / outer
    angle_a = 2.0 * np.pi * np.arange(lanes)[:, None] * np.arange(lanes)[None, :] / lanes
    angle_t = 2.0 * np.pi * np.arange(outer)[:, None] * np.arange(lanes)[None, :] / total
    return dict(
        cos_b=f32(np.cos(angle_b)),
        neg_sin_b=f32(-np.sin(angle_b)),
        cos_a=f32(np.cos(angle_a)),
        sin_a=f32(np.sin(angle_a)),
        cos_t=f32(np.cos(angle_t))[:, None, :],
        sin_t=f32(np.sin(angle_t))[:, None, :],
        inv_cos_b=f32(np.cos(angle_b).T / total),
        inv_sin_b=f32(np.sin(angle_b).T / total),
    )


def mm(spec, a, b):
    return jnp.einsum(spec, a, b, precision=dft_precision, preferred_element_type=jnp.float32)


def forward_dft(data, tab):
    y_re = mm("kn,ncm->kcm", tab["cos_b"], data)
    y_im = mm("kn,ncm->kcm", tab["neg_sin_b"], data)
    tc, ts = tab["cos_t"], tab["sin_t"]
    t_re = y_re * tc + y_im * ts
    t_im = y_im * tc - y_re * ts
    x_re = mm("kcm,am->kca", t_re, tab["cos_a"]) + mm("kcm,am->kca", t_im, tab["sin_a"])
    x_im = mm("kcm,am->kca", t_im, tab["cos_a"]) - mm("kcm,am->kca", t_re, tab["sin_a"])
    return x_re, x_im


def inverse_dft(p_re, p_im, tab):
    z_re = mm("kca,ta->kct", p_re, tab["cos_a"]) - mm("kca,ta->kct", p_im, tab["sin_a"])
    z_im = mm("kca,ta->kct", p_im, tab["cos_a"]) + mm("kca,ta->kct", p_re, tab["sin_a"])
    tc, ts = tab["cos_t"], tab["sin_t"]
    w_re = z_re * tc - z_im * ts
    w_im = z_re * ts + z_im * tc
    return mm("sk,kct->sct", tab["inv_cos_b"], w_re) - mm("sk,kct->sct", tab["inv_sin_b"], w_im)


def on_device(
    hyena_query, hyena_key, hyena_value, bias, groups, filters, att_queries, att_keys, block_mask
):
    rows_dev, channels = hyena_query.shape
    pieces = lax.axis_size("seq")
    device = lax.axis_index("seq")
    length = rows_dev * pieces
    width = channels // pieces
    tab = dft_tables(length)

    mixed = (hyena_key.astype(jnp.float32) * hyena_value.astype(jnp.float32)).astype(jnp.bfloat16)
    halves = rows_dev // 128
    sends = [
        part.reshape(halves, 128, pieces, width).transpose(2, 0, 3, 1)
        for part in (mixed, hyena_query)
    ]
    got = lax.all_to_all(jnp.concatenate(sends, axis=2), "seq", 0, 0, tiled=True)
    got = got.reshape(pieces * halves, 2 * width, 128)
    mixed_cols = got[:, :width]
    query_cols = got[:, width:]

    chan_count = lax.axis_size("chan")
    local = filters.astype(jnp.bfloat16)
    spread = jnp.broadcast_to(local[None], (chan_count,) + local.shape)
    bank = lax.all_to_all(spread, "chan", 0, 0, tiled=True).reshape(-1, local.shape[1])
    picked = jnp.take(bank, groups.reshape(pieces, width), axis=0)
    picked = picked.reshape(pieces, width, halves, 128).transpose(0, 2, 1, 3)
    kernel = lax.all_to_all(picked, "seq", 0, 0, tiled=True).reshape(pieces * halves, width, 128)

    s_re, s_im = forward_dft(mixed_cols, tab)
    f_re, f_im = forward_dft(kernel, tab)
    conv = inverse_dft(s_re * f_re - s_im * f_im, s_re * f_im + s_im * f_re, tab)
    bias_here = lax.dynamic_slice_in_dim(bias, device * width, width)
    out_cols = (
        query_cols.astype(jnp.float32)
        * (conv + bias_here[None, :, None] * mixed_cols.astype(jnp.float32))
    ).astype(jnp.bfloat16)
    back = lax.all_to_all(out_cols.reshape(pieces, halves, width, 128), "seq", 0, 0, tiled=True)
    hyena_out = back.transpose(1, 3, 0, 2).reshape(rows_dev, channels)
    value_t = out_cols.transpose(1, 0, 2).reshape(width, length)

    attn_out = attention(att_queries, att_keys, value_t, block_mask, pieces, device)
    return (hyena_out, attn_out)


def attention(att_queries, att_keys, value_half, block_mask, pieces, device):
    rows_dev, channels = att_queries.shape
    heads = channels // HD
    length = rows_dev * pieces
    sub = rows_dev // ABLK
    parity = device % sub
    head = device // sub

    block_count = block_mask.shape[1]
    queries = att_queries.reshape(sub, ABLK, heads, HD).transpose(2, 0, 1, 3)
    keys = att_keys.reshape(rows_dev, heads, 1, HD).transpose(1, 2, 0, 3)
    keys = jnp.broadcast_to(keys, (heads, sub, rows_dev, HD))
    mask_pad = jnp.zeros((sub, 8, HD), jnp.bfloat16).at[:, 0, :block_count].set(
        block_mask.astype(jnp.bfloat16)
    )
    mask_pad = jnp.broadcast_to(mask_pad[None], (heads, sub, 8, HD))
    payload = jnp.concatenate([keys, queries, mask_pad], axis=2)
    payload = payload.reshape(heads * sub, rows_dev + ABLK + 8, HD)
    got = lax.all_to_all(payload, "seq", 0, 0, tiled=True)
    k_here = got[:, :rows_dev].reshape(length, HD)
    q_here = got[:, rows_dev : rows_dev + ABLK].reshape(pieces * ABLK, HD)
    mask_rows = got[:, rows_dev + ABLK, :block_count] > 0.5

    pairs = [(source, source ^ 1) for source in range(pieces)]
    other_half = lax.ppermute(value_half, "seq", pairs)
    first = jnp.where(parity == 0, value_half, other_half)
    second = jnp.where(parity == 0, other_half, value_half)
    v_here = jnp.concatenate([first, second], axis=0)

    scale = HD ** (-0.5)
    q_blocks = sub * jnp.arange(pieces, dtype=jnp.int32) + parity
    query_pos = (q_blocks[:, None] * ABLK + jnp.arange(ABLK, dtype=jnp.int32)[None, :]).reshape(-1)
    group_count = 4
    per_group = pieces // group_count
    outs = []
    for g in range(group_count):
        rows = slice(g * per_group * ABLK, (g + 1) * per_group * ABLK)
        key_len = length * (g + 1) // group_count
        kblocks = key_len // ABLK
        block_ok = mask_rows[g * per_group : (g + 1) * per_group, :kblocks]
        q_pos = query_pos[rows].reshape(per_group, ABLK)
        k_pos = jnp.arange(key_len, dtype=jnp.int32).reshape(kblocks, ABLK)
        allowed = block_ok[:, None, :, None] & (
            k_pos[None, None, :, :] <= q_pos[:, :, None, None]
        )
        scores = jnp.dot(q_here[rows], k_here[:key_len].T, preferred_element_type=jnp.float32) * scale
        scores = scores.reshape(per_group, ABLK, kblocks, ABLK)
        scores = jnp.where(allowed, scores, -1e30)
        largest = jnp.max(scores, axis=(2, 3), keepdims=True)
        weights = jnp.exp(scores - largest)
        totals = jnp.sum(weights, axis=(2, 3)).reshape(per_group * ABLK, 1)
        weights = weights.reshape(per_group * ABLK, key_len).astype(jnp.bfloat16)
        acc = jnp.einsum("qs,cs->qc", weights, v_here[:, :key_len], preferred_element_type=jnp.float32)
        outs.append(acc / totals)
    result = jnp.concatenate(outs, axis=0).astype(jnp.bfloat16)

    back = lax.all_to_all(result.reshape(pieces, ABLK, HD), "seq", 0, 0, tiled=True)
    back = back.reshape(heads, sub, ABLK, HD).transpose(1, 2, 0, 3)
    return back.reshape(rows_dev, channels)


def solution(mesh):
    return jax.shard_map(
        on_device,
        mesh=mesh,
        in_specs=(
            P("seq", "chan"),
            P("seq", "chan"),
            P("seq", "chan"),
            P("chan"),
            P("chan"),
            P("chan", "seq"),
            P("seq", "chan"),
            P("seq", "chan"),
            P("seq", None),
        ),
        out_specs=(P("seq", "chan"), P("seq", "chan")),
        check_vma=False,
    )
```
